512 devices in a mesh: dp: 16 (over x, y_hi, core), ctx: 32 (over z, y_lo).
Axes of the slice: x: 4, y: 8 (y_hi: 2, y_lo: 4; y = y_hi * 4 + y_lo), z: 8, core: 2. Of those that a mesh axis runs over, the one named last changes fastest.
Arguments:
- queries: bfloat16 [16, 4096, 512], P('dp', 'ctx'), may hold values from -6 to 6
- keys: bfloat16 [16, 4096, 512], P('dp', 'ctx'), may hold values from -6 to 6
- values: bfloat16 [16, 4096, 512], P('dp', 'ctx'), may hold values from -6 to 6
- grad_out: bfloat16 [16, 4096, 8192], P('dp', 'ctx'), may hold values from -6 to 6
- out_weight: bfloat16 [512, 8192], P(None, 'ctx'), may hold values from -0.25 to 0.25
- residues: float32 [512, 16], P('ctx'), may hold values from -0.125 to 0.125
- decays: float32 [512, 16], P('ctx'), may hold values from 1.2207031e-05 to 0.1
Outputs:
- grad_queries: bfloat16 [16, 4096, 512], P('dp', None, 'ctx')
- grad_keys: bfloat16 [16, 4096, 512], P('dp', None, 'ctx')
- grad_values: bfloat16 [16, 4096, 512], P('dp', None, 'ctx')
- grad_weight: float32 [512, 8192], P(None, 'ctx')
- grad_residues: float32 [512, 16], P('ctx')
- grad_decays: float32 [512, 16], P('ctx')
The draws below stay inside these ranges and needn't reach their ends.
All inputs are finite; a program needn't handle non-finite values.
Results may differ from the reference program's by a relative error of at most 0.017.
Values may be sent and summed in bfloat16 or wider, within the bound.
No kernel may reach another device: no remote copies, remote signals or barrier semaphores. Data moves between devices by JAX's collectives and lax.ppermute only.
A program may use at most 128 MiB of HBM per device.

```python
import math
import jax
import jax.numpy as jnp
from jax import lax

D = 8192
C = 512
ORDER = 16
SEQ = 4096
BATCH = 16
N_CTX = 32


def level_of(key, dims, split, least, high):
    def one(dim, shards_of):
        draws = jax.random.uniform(jax.random.fold_in(jax.random.fold_in(key, 6), dim), (shards_of,), jnp.float32, least / len(split), high / len(split))
        return jnp.repeat(jnp.exp(draws), dims[dim] // shards_of).reshape((-1,) + (1,) * (len(dims) - dim - 1))

    gain = one(*split[0])
    for cut in split[1:]:
        gain = gain * one(*cut)
    return gain


def normal_values(stream_key, extent, deviation, reach, pieces=(), dtype=jnp.bfloat16):
    level = level_of(stream_key, extent, pieces, -0.22, 0.18) if pieces else 1.0
    array = jax.random.normal(stream_key, extent, jnp.float32) * deviation * level
    return jnp.minimum(jnp.maximum(array, -reach), reach).astype(dtype)


def setup_inputs(seed: int = 0) -> dict:
    arg_keys = jax.random.split(jax.random.key(seed), 8)
    queries = normal_values(arg_keys[0], (BATCH, SEQ, C), 1.0, 6.0, ((0, 16), (1, 32)))
    keys = normal_values(arg_keys[1], (BATCH, SEQ, C), 1.0, 6.0, ((0, 16), (1, 32)))
    values = normal_values(arg_keys[2], (BATCH, SEQ, C), 1.0, 6.0, ((0, 16), (1, 32)))
    grad_out = normal_values(arg_keys[3], (BATCH, SEQ, D), 1.0, 6.0, ((0, 16), (1, 32)))
    out_weight = normal_values(arg_keys[4], (C, D), C ** -0.5, 0.25, ((1, 32),))
    residues = normal_values(arg_keys[5], (C, ORDER), (2.0 / (ORDER * SEQ) ** 0.5), 0.125, ((0, 32),), jnp.float32)
    decays = jnp.clip(jnp.exp(math.log(0.1) - 9.010913 * jax.random.uniform(arg_keys[6], (C, ORDER), jnp.float32) ** level_of(arg_keys[6], (C, ORDER), ((0, 32),), -0.2, 0.2)), 1.220703143189894e-05, 0.1)
    return {"queries": queries, "keys": keys, "values": values, "grad_out": grad_out, "out_weight": out_weight, "residues": residues, "decays": decays}


def reference(queries, keys, values, grad_out, out_weight, residues, decays):
    positions = jnp.arange(SEQ).astype(jnp.float32)
    decay_terms = jnp.exp(-decays[None, :, :] * positions[:, None, None])
    filter_taps = jnp.sum(residues[None, :, :] * decay_terms, axis=2)
    length = 2 * SEQ
    filter_freq = jnp.fft.rfft(filter_taps, n=length, axis=0)
    block_width = D // N_CTX

    def one_sequence(carry, items):
        weight_sum, taps_sum = carry
        query_rows, key_rows, value_rows, grad_rows = items

        def add_block(index, total):
            offset = (index * block_width).astype(jnp.int32)
            grad_part = lax.dynamic_slice_in_dim(grad_rows, offset, block_width, 1)
            weight_part = lax.dynamic_slice_in_dim(out_weight, offset, block_width, 1)
            term = jnp.dot(grad_part, weight_part.T, preferred_element_type=jnp.float32).astype(jnp.bfloat16)
            term = lax.optimization_barrier(term)
            return total + term.astype(jnp.float32)

        gated_sum = lax.fori_loop(0, N_CTX, add_block, jnp.zeros((SEQ, C), jnp.float32))
        grad_gated = gated_sum.astype(jnp.bfloat16)
        query_full = query_rows.astype(jnp.float32)
        key_full = key_rows.astype(jnp.float32)
        value_full = value_rows.astype(jnp.float32)
        product = key_full * value_full
        prod_freq = jnp.fft.rfft(product, n=length, axis=0)
        conv_out = jnp.fft.irfft(prod_freq * filter_freq, n=length, axis=0)[:SEQ]
        gated = (query_full * conv_out).astype(jnp.bfloat16)
        grad_queries = (grad_gated.astype(jnp.float32) * conv_out).astype(jnp.bfloat16)
        grad_conv = grad_gated.astype(jnp.float32) * query_full
        grad_freq = jnp.fft.rfft(grad_conv, n=length, axis=0)
        grad_product = jnp.fft.irfft(jnp.conj(filter_freq) * grad_freq, n=length, axis=0)[:SEQ]
        grad_taps = jnp.fft.irfft(jnp.conj(prod_freq) * grad_freq, n=length, axis=0)[:SEQ]
        grad_keys = (grad_product * value_full).astype(jnp.bfloat16)
        grad_values = (grad_product * key_full).astype(jnp.bfloat16)
        weight_sum = weight_sum + jnp.dot(gated.T, grad_rows, preferred_element_type=jnp.float32)
        taps_sum = taps_sum + grad_taps
        return (weight_sum, taps_sum), (grad_queries, grad_keys, grad_values)

    start = (jnp.zeros((C, D), jnp.float32), jnp.zeros((SEQ, C), jnp.float32))
    (grad_weight, taps_sum), (grad_queries, grad_keys, grad_values) = lax.scan(
        one_sequence, start, (queries, keys, values, grad_out))
    grad_residues = jnp.sum(taps_sum[:, :, None] * decay_terms, axis=0)
    grad_decays = -residues * jnp.sum((taps_sum * positions[:, None])[:, :, None] * decay_terms, axis=0)
    return grad_queries, grad_keys, grad_values, grad_weight, grad_residues, grad_decays
```

```python
import math

import jax
import jax.numpy as jnp
from jax import lax
from jax.sharding import PartitionSpec as P

FFT_COLS = 128


HIGHEST = lax.Precision.HIGHEST


def fourier_tables(fft_rows, fft_cols):
    total = fft_rows * fft_cols
    row_index = jnp.arange(fft_rows, dtype=jnp.int32)
    col_index = jnp.arange(fft_cols, dtype=jnp.int32)
    first = (row_index[:, None] * row_index[None, :] % fft_rows).astype(jnp.float32) * (
        2.0 * math.pi / fft_rows
    )
    twist = (row_index[:, None] * col_index[None, :] % total).astype(jnp.float32) * (
        2.0 * math.pi / total
    )
    second = (col_index[:, None] * col_index[None, :] % fft_cols).astype(jnp.float32) * (
        2.0 * math.pi / fft_cols
    )
    return (
        (jnp.cos(first), -jnp.sin(first)),
        (jnp.cos(twist), -jnp.sin(twist)),
        (jnp.cos(second), -jnp.sin(second)),
    )


def complex_product(left_re, left_im, right_re, right_im):
    return (left_re * right_re - left_im * right_im, left_re * right_im + left_im * right_re)


def apply_middle(table_re, table_im, data_re):

    def single(table, data):
        return jnp.einsum("kn,cnm->ckm", table, data, precision=HIGHEST)

    return (single(table_re, data_re), single(table_im, data_re))


def apply_last(table_re, table_im, data_re, data_im):

    def single(data, table):
        return jnp.einsum("ckm,mj->ckj", data, table, precision=HIGHEST)

    return (
        single(data_re, table_re) - single(data_im, table_im),
        single(data_im, table_re) + single(data_re, table_im),
    )


def forward_transform(signal, tables):
    (first_re, first_im), (twist_re, twist_im), (second_re, second_im) = tables
    section_re, section_im = apply_middle(first_re, first_im, signal)
    section_re, section_im = complex_product(section_re, section_im, twist_re, twist_im)
    return apply_last(second_re, second_im, section_re, section_im)


def inverse_transform(spec_re, spec_im, tables):
    (first_re, first_im), (twist_re, twist_im), (second_re, second_im) = tables
    section_re, section_im = apply_last(second_re, -second_im, spec_re, spec_im)
    section_re, section_im = complex_product(section_re, section_im, twist_re, -twist_im)
    result = jnp.einsum("kn,cnm->ckm", first_re, section_re, precision=HIGHEST) + jnp.einsum(
        "kn,cnm->ckm", first_im, section_im, precision=HIGHEST
    )
    total = first_re.shape[0] * second_re.shape[0]
    return result / float(total)


def padded_grid(signal, fft_rows, fft_cols):
    channels, seq_len = signal.shape
    padded = jnp.concatenate(
        [signal, jnp.zeros((channels, fft_rows * fft_cols - seq_len), jnp.float32)], axis=1
    )
    return padded.reshape(channels, fft_rows, fft_cols)


def leading_part(grid, seq_len):
    return grid.reshape(grid.shape[0], -1)[:, :seq_len]


def channels_first(block):
    return block[0].astype(jnp.float32).T


def rounded_sum(terms):
    rounded = lax.optimization_barrier(terms.astype(jnp.bfloat16))
    return jnp.sum(rounded.astype(jnp.float32), axis=0)


def axis_pairs(size, mask):
    return [(index, index ^ mask) for index in range(size)]


def ctx_masks(size):
    bits = [1 << b for b in range(size.bit_length() - 1)]
    low = [m for m in bits if m < 4]
    high = [m for m in bits if m >= 4]
    return tuple(reversed(high[1:])) + tuple(reversed(low[1:])) + tuple(high[:1]) + tuple(low[:1])


def doubling_gather(block, axis, masks):
    size = lax.axis_size(axis)
    held = block
    for mask in masks:
        held = jnp.concatenate([held, lax.ppermute(held, axis, axis_pairs(size, mask))], axis=0)
    return held


def unpermute_blocks(rows, axis, masks):
    size = lax.axis_size(axis)
    me = lax.axis_index(axis)
    wanted = me ^ jnp.arange(size, dtype=jnp.int32)
    place = jnp.zeros_like(wanted)
    for step, mask in enumerate(masks):
        place = place | (((wanted & mask) != 0).astype(jnp.int32) << step)
    blocks = rows.reshape(size, rows.shape[0] // size, rows.shape[1])
    return jnp.take(blocks, place, axis=0).reshape(rows.shape)


def dp_masks(size):
    bits = [1 << b for b in range(size.bit_length() - 1)]
    return tuple(bits[:1]) + tuple(bits[2:]) + tuple(bits[1:2])


def summed_over_dp(grad_weight, grad_residues, grad_decays):
    size = lax.axis_size("dp")
    width = grad_weight.shape[1]
    extra = jnp.stack([grad_residues.reshape(-1), grad_decays.reshape(-1)])
    extra = jnp.pad(extra, ((0, 0), (0, width - extra.shape[1])))
    rows = grad_weight.shape[0] + 2
    padded_rows = -(-rows // size) * size
    held = jnp.concatenate(
        [grad_weight, extra, jnp.zeros((padded_rows - rows, width), jnp.float32)], axis=0
    )
    me = lax.axis_index("dp")
    masks = dp_masks(size)
    for mask in masks:
        half = held.shape[0] // 2
        low, high = held[:half], held[half:]
        upper = (me & mask) != 0
        keep = jnp.where(upper, high, low)
        send = jnp.where(upper, low, high)
        held = keep + lax.ppermute(send, "dp", axis_pairs(size, mask))
    for mask in reversed(masks):
        other = lax.ppermute(held, "dp", axis_pairs(size, mask))
        upper = (me & mask) != 0
        held = jnp.where(upper, jnp.concatenate([other, held]), jnp.concatenate([held, other]))
    count = grad_residues.size
    weight = held[: grad_weight.shape[0]]
    residue_sum = held[grad_weight.shape[0], :count].reshape(grad_residues.shape)
    decay_sum = held[grad_weight.shape[0] + 1, :count].reshape(grad_decays.shape)
    return weight, residue_sum, decay_sum


def body(queries, keys, values, grad_out, out_weight, residues, decays):
    channels = out_weight.shape[0]
    block_width = out_weight.shape[1]
    tok_rows = grad_out.shape[1]
    grad_cols = lax.all_to_all(grad_out, "ctx", split_axis=2, concat_axis=1, tiled=True)
    shard_piece = lax.all_gather(out_weight, "ctx", axis=1, tiled=True)
    blocks = shard_piece.shape[1] // block_width
    partial_value = grad_out[0]
    partial_value = partial_value.reshape(tok_rows, blocks, block_width)
    weight_part = shard_piece.reshape(channels, blocks, block_width)
    terms = jnp.einsum(
        "tks,cks->ktc", partial_value, weight_part, preferred_element_type=jnp.float32
    )
    gated_sum = rounded_sum(terms)
    grad_gated = gated_sum.astype(jnp.bfloat16)[None]
    query_ch, key_ch, value_ch, gated_grad_ch = (
        lax.all_to_all(queries, "ctx", split_axis=2, concat_axis=1, tiled=True),
        lax.all_to_all(keys, "ctx", split_axis=2, concat_axis=1, tiled=True),
        lax.all_to_all(values, "ctx", split_axis=2, concat_axis=1, tiled=True),
        lax.all_to_all(grad_gated, "ctx", split_axis=2, concat_axis=1, tiled=True),
    )
    grad_gated_full = channels_first(gated_grad_ch)
    seq_len = query_ch.shape[1]
    fft_rows = 2 * seq_len // FFT_COLS
    tables = fourier_tables(fft_rows, FFT_COLS)
    query_full = channels_first(query_ch)
    key_full = channels_first(key_ch)
    value_full = channels_first(value_ch)
    positions = jnp.arange(seq_len).astype(jnp.float32)
    decay_terms = jnp.exp(-decays[:, :, None] * positions[None, None, :])
    filter_taps = jnp.sum(residues[:, :, None] * decay_terms, axis=1)
    product = key_full * value_full
    grad_conv = grad_gated_full * query_full
    prod_re, prod_im = forward_transform(padded_grid(product, fft_rows, FFT_COLS), tables)
    taps_re, taps_im = forward_transform(padded_grid(filter_taps, fft_rows, FFT_COLS), tables)
    grad_re, grad_im = forward_transform(padded_grid(grad_conv, fft_rows, FFT_COLS), tables)
    conv_out = leading_part(
        inverse_transform(*complex_product(prod_re, prod_im, taps_re, taps_im), tables), seq_len
    )
    grad_product = leading_part(
        inverse_transform(*complex_product(taps_re, -taps_im, grad_re, grad_im), tables), seq_len
    )
    grad_taps = leading_part(
        inverse_transform(*complex_product(prod_re, -prod_im, grad_re, grad_im), tables), seq_len
    )
    gated_t = (query_full * conv_out).astype(jnp.bfloat16)
    grad_queries = (grad_gated_full * conv_out).T.astype(jnp.bfloat16)[None]
    grad_keys = (grad_product * value_full).T.astype(jnp.bfloat16)[None]
    grad_values = (grad_product * key_full).T.astype(jnp.bfloat16)[None]
    ctx_size = lax.axis_size("ctx")
    gather_masks = ctx_masks(ctx_size)
    gathered = doubling_gather(gated_t, "ctx", gather_masks)
    partial_value = lax.dot_general(
        gathered,
        grad_cols[0],
        (((1,), (0,)), ((), ())),
        preferred_element_type=jnp.float32,
    )
    grad_weight = unpermute_blocks(partial_value, "ctx", gather_masks)
    grad_residues = jnp.sum(grad_taps[:, None, :] * decay_terms, axis=2)
    grad_decays = -residues * jnp.sum(
        (grad_taps * positions[None, :])[:, None, :] * decay_terms, axis=2
    )
    grad_weight, grad_residues, grad_decays = summed_over_dp(
        grad_weight, grad_residues, grad_decays
    )
    return (grad_queries, grad_keys, grad_values, grad_weight, grad_residues, grad_decays)


def solution(mesh):
    placed = (
        P("dp", "ctx", None),
        P("dp", "ctx", None),
        P("dp", "ctx", None),
        P("dp", "ctx", None),
        P(None, "ctx"),
        P("ctx", None),
        P("ctx", None),
    )
    return jax.shard_map(
        body,
        mesh=mesh,
        in_specs=placed,
        out_specs=(
            P("dp", None, "ctx"),
            P("dp", None, "ctx"),
            P("dp", None, "ctx"),
            P(None, "ctx"),
            P("ctx", None),
            P("ctx", None),
        ),
        check_vma=False,
    )
```

```python
import math

import jax
import jax.numpy as jnp
from jax import lax
from jax.sharding import PartitionSpec as P

FFT_COLS = 128


HIGHEST = lax.Precision.HIGHEST


def fourier_tables(fft_rows, fft_cols):
    total = fft_rows * fft_cols
    row_index = jnp.arange(fft_rows, dtype=jnp.int32)
    col_index = jnp.arange(fft_cols, dtype=jnp.int32)
    first = (row_index[:, None] * row_index[None, :] % fft_rows).astype(jnp.float32) * (
        2.0 * math.pi / fft_rows
    )
    twist = (row_index[:, None] * col_index[None, :] % total).astype(jnp.float32) * (
        2.0 * math.pi / total
    )
    second = (col_index[:, None] * col_index[None, :] % fft_cols).astype(jnp.float32) * (
        2.0 * math.pi / fft_cols
    )
    return (
        (jnp.cos(first), -jnp.sin(first)),
        (jnp.cos(twist), -jnp.sin(twist)),
        (jnp.cos(second), -jnp.sin(second)),
    )


def complex_product(left_re, left_im, right_re, right_im):
    return (left_re * right_re - left_im * right_im, left_re * right_im + left_im * right_re)


def apply_middle(table_re, table_im, data_re):

    def single(table, data):
        return jnp.einsum("kn,cnm->ckm", table, data, precision=HIGHEST)

    return (single(table_re, data_re), single(table_im, data_re))


def apply_last(table_re, table_im, data_re, data_im):

    def single(data, table):
        return jnp.einsum("ckm,mj->ckj", data, table, precision=HIGHEST)

    return (
        single(data_re, table_re) - single(data_im, table_im),
        single(data_im, table_re) + single(data_re, table_im),
    )


def forward_transform(signal, tables):
    (first_re, first_im), (twist_re, twist_im), (second_re, second_im) = tables
    section_re, section_im = apply_middle(first_re, first_im, signal)
    section_re, section_im = complex_product(section_re, section_im, twist_re, twist_im)
    return apply_last(second_re, second_im, section_re, section_im)


def inverse_transform(spec_re, spec_im, tables):
    (first_re, first_im), (twist_re, twist_im), (second_re, second_im) = tables
    section_re, section_im = apply_last(second_re, -second_im, spec_re, spec_im)
    section_re, section_im = complex_product(section_re, section_im, twist_re, -twist_im)
    result = jnp.einsum("kn,cnm->ckm", first_re, section_re, precision=HIGHEST) + jnp.einsum(
        "kn,cnm->ckm", first_im, section_im, precision=HIGHEST
    )
    total = first_re.shape[0] * second_re.shape[0]
    return result / float(total)


def padded_grid(signal, fft_rows, fft_cols):
    channels, seq_len = signal.shape
    padded = jnp.concatenate(
        [signal, jnp.zeros((channels, fft_rows * fft_cols - seq_len), jnp.float32)], axis=1
    )
    return padded.reshape(channels, fft_rows, fft_cols)


def leading_part(grid, seq_len):
    return grid.reshape(grid.shape[0], -1)[:, :seq_len]


def channels_first(block):
    return block[0].astype(jnp.float32).T


def rounded_sum(terms):
    rounded = lax.optimization_barrier(terms.astype(jnp.bfloat16))
    return jnp.sum(rounded.astype(jnp.float32), axis=0)


def columns_by_position(rows, block_width):
    tok_rows = rows.shape[0]
    blocks = rows.shape[1] // block_width
    pieces = jnp.transpose(rows.reshape(tok_rows, blocks, block_width), (1, 0, 2))
    moved = lax.all_to_all(pieces, "ctx", split_axis=0, concat_axis=0, tiled=True)
    return moved.reshape(blocks * tok_rows, block_width)


def axis_pairs(size, mask):
    return [(index, index ^ mask) for index in range(size)]


def ctx_masks(size):
    bits = [1 << b for b in range(size.bit_length() - 1)]
    low = [m for m in bits if m < 4]
    high = [m for m in bits if m >= 4]
    return tuple(reversed(high[1:])) + tuple(reversed(low[1:])) + tuple(high[:1]) + tuple(low[:1])


def doubling_gather(block, axis, masks):
    size = lax.axis_size(axis)
    held = block
    for mask in masks:
        held = jnp.concatenate([held, lax.ppermute(held, axis, axis_pairs(size, mask))], axis=0)
    return held


def unpermute_blocks(rows, axis, masks):
    size = lax.axis_size(axis)
    me = lax.axis_index(axis)
    wanted = me ^ jnp.arange(size, dtype=jnp.int32)
    place = jnp.zeros_like(wanted)
    for step, mask in enumerate(masks):
        place = place | (((wanted & mask) != 0).astype(jnp.int32) << step)
    blocks = rows.reshape(size, rows.shape[0] // size, rows.shape[1])
    return jnp.take(blocks, place, axis=0).reshape(rows.shape)


def dp_masks(size):
    bits = [1 << b for b in range(size.bit_length() - 1)]
    return tuple(bits[:1]) + tuple(bits[2:]) + tuple(bits[1:2])


def summed_over_dp(grad_weight, grad_residues, grad_decays):
    size = lax.axis_size("dp")
    width = grad_weight.shape[1]
    extra = jnp.stack([grad_residues.reshape(-1), grad_decays.reshape(-1)])
    extra = jnp.pad(extra, ((0, 0), (0, width - extra.shape[1])))
    rows = grad_weight.shape[0] + 2
    padded_rows = -(-rows // size) * size
    held = jnp.concatenate(
        [grad_weight, extra, jnp.zeros((padded_rows - rows, width), jnp.float32)], axis=0
    )
    me = lax.axis_index("dp")
    masks = dp_masks(size)
    for mask in masks:
        half = held.shape[0] // 2
        low, high = held[:half], held[half:]
        upper = (me & mask) != 0
        keep = jnp.where(upper, high, low)
        send = jnp.where(upper, low, high)
        held = keep + lax.ppermute(send, "dp", axis_pairs(size, mask))
    for mask in reversed(masks):
        other = lax.ppermute(held, "dp", axis_pairs(size, mask))
        upper = (me & mask) != 0
        held = jnp.where(upper, jnp.concatenate([other, held]), jnp.concatenate([held, other]))
    count = grad_residues.size
    weight = held[: grad_weight.shape[0]]
    residue_sum = held[grad_weight.shape[0], :count].reshape(grad_residues.shape)
    decay_sum = held[grad_weight.shape[0] + 1, :count].reshape(grad_decays.shape)
    return weight, residue_sum, decay_sum


def body(queries, keys, values, grad_out, out_weight, residues, decays):
    channels = out_weight.shape[0]
    block_width = out_weight.shape[1]
    tok_rows = grad_out.shape[1]
    shard_piece = lax.all_gather(out_weight, "ctx", axis=1, tiled=True)
    grad_cols = columns_by_position(grad_out[0], block_width)
    shard_piece, grad_cols = lax.optimization_barrier((shard_piece, grad_cols))
    blocks = shard_piece.shape[1] // block_width
    partial_value = grad_out[0]
    partial_value = partial_value.reshape(tok_rows, blocks, block_width)
    weight_part = shard_piece.reshape(channels, blocks, block_width)
    terms = jnp.einsum(
        "tks,cks->ktc", partial_value, weight_part, preferred_element_type=jnp.float32
    )
    gated_sum = rounded_sum(terms)
    grad_gated = gated_sum.astype(jnp.bfloat16)[None]
    query_ch, key_ch, value_ch, gated_grad_ch = (
        lax.all_to_all(queries, "ctx", split_axis=2, concat_axis=1, tiled=True),
        lax.all_to_all(keys, "ctx", split_axis=2, concat_axis=1, tiled=True),
        lax.all_to_all(values, "ctx", split_axis=2, concat_axis=1, tiled=True),
        lax.all_to_all(grad_gated, "ctx", split_axis=2, concat_axis=1, tiled=True),
    )
    grad_gated_full = channels_first(gated_grad_ch)
    seq_len = query_ch.shape[1]
    fft_rows = 2 * seq_len // FFT_COLS
    tables = fourier_tables(fft_rows, FFT_COLS)
    query_full = channels_first(query_ch)
    key_full = channels_first(key_ch)
    value_full = channels_first(value_ch)
    positions = jnp.arange(seq_len).astype(jnp.float32)
    decay_terms = jnp.exp(-decays[:, :, None] * positions[None, None, :])
    filter_taps = jnp.sum(residues[:, :, None] * decay_terms, axis=1)
    product = key_full * value_full
    grad_conv = grad_gated_full * query_full
    prod_re, prod_im = forward_transform(padded_grid(product, fft_rows, FFT_COLS), tables)
    taps_re, taps_im = forward_transform(padded_grid(filter_taps, fft_rows, FFT_COLS), tables)
    grad_re, grad_im = forward_transform(padded_grid(grad_conv, fft_rows, FFT_COLS), tables)
    conv_out = leading_part(
        inverse_transform(*complex_product(prod_re, prod_im, taps_re, taps_im), tables), seq_len
    )
    grad_product = leading_part(
        inverse_transform(*complex_product(taps_re, -taps_im, grad_re, grad_im), tables), seq_len
    )
    grad_taps = leading_part(
        inverse_transform(*complex_product(prod_re, -prod_im, grad_re, grad_im), tables), seq_len
    )
    gated_t = (query_full * conv_out).astype(jnp.bfloat16)
    grad_queries = (grad_gated_full * conv_out).T.astype(jnp.bfloat16)[None]
    grad_keys = (grad_product * value_full).T.astype(jnp.bfloat16)[None]
    grad_values = (grad_product * key_full).T.astype(jnp.bfloat16)[None]
    ctx_size = lax.axis_size("ctx")
    gather_masks = ctx_masks(ctx_size)
    gathered = doubling_gather(gated_t, "ctx", gather_masks)
    partial_value = lax.dot_general(
        gathered,
        grad_cols,
        (((1,), (0,)), ((), ())),
        preferred_element_type=jnp.float32,
    )
    grad_weight = unpermute_blocks(partial_value, "ctx", gather_masks)
    grad_residues = jnp.sum(grad_taps[:, None, :] * decay_terms, axis=2)
    grad_decays = -residues * jnp.sum(
        (grad_taps * positions[None, :])[:, None, :] * decay_terms, axis=2
    )
    grad_weight, grad_residues, grad_decays = summed_over_dp(
        grad_weight, grad_residues, grad_decays
    )
    return (grad_queries, grad_keys, grad_values, grad_weight, grad_residues, grad_decays)


def solution(mesh):
    placed = (
        P("dp", "ctx", None),
        P("dp", "ctx", None),
        P("dp", "ctx", None),
        P("dp", "ctx", None),
        P(None, "ctx"),
        P("ctx", None),
        P("ctx", None),
    )
    return jax.shard_map(
        body,
        mesh=mesh,
        in_specs=placed,
        out_specs=(
            P("dp", None, "ctx"),
            P("dp", None, "ctx"),
            P("dp", None, "ctx"),
            P(None, "ctx"),
            P("ctx", None),
            P("ctx", None),
        ),
        check_vma=False,
    )
```

```python
import math

import jax
import jax.numpy as jnp
from jax import lax
from jax.sharding import PartitionSpec as P

FFT_COLS = 128


HIGHEST = lax.Precision.HIGHEST


def fourier_tables(fft_rows, fft_cols):
    total = fft_rows * fft_cols
    row_index = jnp.arange(fft_rows, dtype=jnp.int32)
    col_index = jnp.arange(fft_cols, dtype=jnp.int32)
    first = (row_index[:, None] * row_index[None, :] % fft_rows).astype(jnp.float32) * (
        2.0 * math.pi / fft_rows
    )
    twist = (row_index[:, None] * col_index[None, :] % total).astype(jnp.float32) * (
        2.0 * math.pi / total
    )
    second = (col_index[:, None] * col_index[None, :] % fft_cols).astype(jnp.float32) * (
        2.0 * math.pi / fft_cols
    )
    return (
        (jnp.cos(first), -jnp.sin(first)),
        (jnp.cos(twist), -jnp.sin(twist)),
        (jnp.cos(second), -jnp.sin(second)),
    )


def complex_product(left_re, left_im, right_re, right_im):
    return (left_re * right_re - left_im * right_im, left_re * right_im + left_im * right_re)


def apply_middle(table_re, table_im, data_re):

    def single(table, data):
        return jnp.einsum("kn,cnm->ckm", table, data, precision=HIGHEST)

    return (single(table_re, data_re), single(table_im, data_re))


def apply_last(table_re, table_im, data_re, data_im):

    def single(data, table):
        return jnp.einsum("ckm,mj->ckj", data, table, precision=HIGHEST)

    return (
        single(data_re, table_re) - single(data_im, table_im),
        single(data_im, table_re) + single(data_re, table_im),
    )


def forward_transform(signal, tables):
    (first_re, first_im), (twist_re, twist_im), (second_re, second_im) = tables
    section_re, section_im = apply_middle(first_re, first_im, signal)
    section_re, section_im = complex_product(section_re, section_im, twist_re, twist_im)
    return apply_last(second_re, second_im, section_re, section_im)


def inverse_transform(spec_re, spec_im, tables):
    (first_re, first_im), (twist_re, twist_im), (second_re, second_im) = tables
    section_re, section_im = apply_last(second_re, -second_im, spec_re, spec_im)
    section_re, section_im = complex_product(section_re, section_im, twist_re, -twist_im)
    result = jnp.einsum("kn,cnm->ckm", first_re, section_re, precision=HIGHEST) + jnp.einsum(
        "kn,cnm->ckm", first_im, section_im, precision=HIGHEST
    )
    total = first_re.shape[0] * second_re.shape[0]
    return result / float(total)


def padded_grid(signal, fft_rows, fft_cols):
    channels, seq_len = signal.shape
    padded = jnp.concatenate(
        [signal, jnp.zeros((channels, fft_rows * fft_cols - seq_len), jnp.float32)], axis=1
    )
    return padded.reshape(channels, fft_rows, fft_cols)


def leading_part(grid, seq_len):
    return grid.reshape(grid.shape[0], -1)[:, :seq_len]


def channels_first(block):
    return block[0].astype(jnp.float32).T


def rounded_sum(terms):
    rounded = lax.optimization_barrier(terms.astype(jnp.bfloat16))
    return jnp.sum(rounded.astype(jnp.float32), axis=0)


def columns_by_position(rows, block_width):
    tok_rows = rows.shape[0]
    blocks = rows.shape[1] // block_width
    pieces = jnp.transpose(rows.reshape(tok_rows, blocks, block_width), (1, 0, 2))
    moved = lax.all_to_all(pieces, "ctx", split_axis=0, concat_axis=0, tiled=True)
    return moved.reshape(blocks * tok_rows, block_width)


def shared_weight(out_weight, masks):
    channels, width = out_weight.shape
    half = width // 2
    core = lax.axis_index("dp") % 2
    piece = lax.dynamic_slice_in_dim(out_weight, core * half, half, axis=1)
    held = doubling_gather(piece, "ctx", masks)
    held = held.reshape(-1, channels, half)
    other = lax.ppermute(held, "dp", axis_pairs(lax.axis_size("dp"), 1))
    return jnp.concatenate([held, other], axis=2)


def matching_columns(rows, blocks, masks):
    tok_rows = rows.shape[0]
    half = rows.shape[1] // (2 * blocks)
    me = lax.axis_index("ctx")
    core = lax.axis_index("dp") % 2
    place = jnp.arange(blocks, dtype=jnp.int32)
    source = jnp.zeros_like(place)
    for step, mask in enumerate(masks):
        source = source | jnp.where(((place >> step) & 1) != 0, mask, 0)
    source = me ^ source
    index = (source[:, None] * 2 + (jnp.arange(2, dtype=jnp.int32)[None, :] ^ core)).reshape(-1)
    halves = jnp.take(rows.reshape(tok_rows, 2 * blocks, half), index, axis=1)
    return halves.reshape(tok_rows, blocks, 2 * half)


def axis_pairs(size, mask):
    return [(index, index ^ mask) for index in range(size)]


def ctx_masks(size):
    bits = [1 << b for b in range(size.bit_length() - 1)]
    low = [m for m in bits if m < 4]
    high = [m for m in bits if m >= 4]
    return tuple(reversed(high[1:])) + tuple(reversed(low[1:])) + tuple(high[:1]) + tuple(low[:1])


def doubling_gather(block, axis, masks):
    size = lax.axis_size(axis)
    held = block
    for mask in masks:
        held = jnp.concatenate([held, lax.ppermute(held, axis, axis_pairs(size, mask))], axis=0)
    return held


def unpermute_blocks(rows, axis, masks):
    size = lax.axis_size(axis)
    me = lax.axis_index(axis)
    wanted = me ^ jnp.arange(size, dtype=jnp.int32)
    place = jnp.zeros_like(wanted)
    for step, mask in enumerate(masks):
        place = place | (((wanted & mask) != 0).astype(jnp.int32) << step)
    blocks = rows.reshape(size, rows.shape[0] // size, rows.shape[1])
    return jnp.take(blocks, place, axis=0).reshape(rows.shape)


def dp_masks(size):
    bits = [1 << b for b in range(size.bit_length() - 1)]
    return tuple(bits[:1]) + tuple(bits[2:]) + tuple(bits[1:2])


def summed_over_dp(grad_weight, grad_residues, grad_decays):
    size = lax.axis_size("dp")
    width = grad_weight.shape[1]
    extra = jnp.stack([grad_residues.reshape(-1), grad_decays.reshape(-1)])
    extra = jnp.pad(extra, ((0, 0), (0, width - extra.shape[1])))
    rows = grad_weight.shape[0] + 2
    padded_rows = -(-rows // size) * size
    held = jnp.concatenate(
        [grad_weight, extra, jnp.zeros((padded_rows - rows, width), jnp.float32)], axis=0
    )
    me = lax.axis_index("dp")
    masks = dp_masks(size)
    for mask in masks:
        half = held.shape[0] // 2
        low, high = held[:half], held[half:]
        upper = (me & mask) != 0
        keep = jnp.where(upper, high, low)
        send = jnp.where(upper, low, high)
        held = keep + lax.ppermute(send, "dp", axis_pairs(size, mask))
    for mask in reversed(masks):
        other = lax.ppermute(held, "dp", axis_pairs(size, mask))
        upper = (me & mask) != 0
        held = jnp.where(upper, jnp.concatenate([other, held]), jnp.concatenate([held, other]))
    count = grad_residues.size
    weight = held[: grad_weight.shape[0]]
    residue_sum = held[grad_weight.shape[0], :count].reshape(grad_residues.shape)
    decay_sum = held[grad_weight.shape[0] + 1, :count].reshape(grad_decays.shape)
    return weight, residue_sum, decay_sum


def body(queries, keys, values, grad_out, out_weight, residues, decays):
    channels = out_weight.shape[0]
    block_width = out_weight.shape[1]
    tok_rows = grad_out.shape[1]
    ctx_size = lax.axis_size("ctx")
    gather_masks = ctx_masks(ctx_size)
    weight_part = shared_weight(out_weight, gather_masks)
    grad_cols = columns_by_position(grad_out[0], block_width)
    weight_part, grad_cols = lax.optimization_barrier((weight_part, grad_cols))
    blocks = weight_part.shape[0]
    partial_value = matching_columns(grad_out[0], blocks, gather_masks)
    terms = jnp.einsum(
        "tks,kcs->ktc", partial_value, weight_part, preferred_element_type=jnp.float32
    )
    gated_sum = rounded_sum(terms)
    grad_gated = gated_sum.astype(jnp.bfloat16)[None]
    query_ch, key_ch, value_ch, gated_grad_ch = (
        lax.all_to_all(queries, "ctx", split_axis=2, concat_axis=1, tiled=True),
        lax.all_to_all(keys, "ctx", split_axis=2, concat_axis=1, tiled=True),
        lax.all_to_all(values, "ctx", split_axis=2, concat_axis=1, tiled=True),
        lax.all_to_all(grad_gated, "ctx", split_axis=2, concat_axis=1, tiled=True),
    )
    grad_gated_full = channels_first(gated_grad_ch)
    seq_len = query_ch.shape[1]
    fft_rows = 2 * seq_len // FFT_COLS
    tables = fourier_tables(fft_rows, FFT_COLS)
    query_full = channels_first(query_ch)
    key_full = channels_first(key_ch)
    value_full = channels_first(value_ch)
    positions = jnp.arange(seq_len).astype(jnp.float32)
    decay_terms = jnp.exp(-decays[:, :, None] * positions[None, None, :])
    filter_taps = jnp.sum(residues[:, :, None] * decay_terms, axis=1)
    product = key_full * value_full
    grad_conv = grad_gated_full * query_full
    prod_re, prod_im = forward_transform(padded_grid(product, fft_rows, FFT_COLS), tables)
    taps_re, taps_im = forward_transform(padded_grid(filter_taps, fft_rows, FFT_COLS), tables)
    grad_re, grad_im = forward_transform(padded_grid(grad_conv, fft_rows, FFT_COLS), tables)
    conv_out = leading_part(
        inverse_transform(*complex_product(prod_re, prod_im, taps_re, taps_im), tables), seq_len
    )
    grad_product = leading_part(
        inverse_transform(*complex_product(taps_re, -taps_im, grad_re, grad_im), tables), seq_len
    )
    grad_taps = leading_part(
        inverse_transform(*complex_product(prod_re, -prod_im, grad_re, grad_im), tables), seq_len
    )
    gated_t = (query_full * conv_out).astype(jnp.bfloat16)
    grad_queries = (grad_gated_full * conv_out).T.astype(jnp.bfloat16)[None]
    grad_keys = (grad_product * value_full).T.astype(jnp.bfloat16)[None]
    grad_values = (grad_product * key_full).T.astype(jnp.bfloat16)[None]
    gathered = doubling_gather(gated_t, "ctx", gather_masks)
    partial_value = lax.dot_general(
        gathered,
        grad_cols,
        (((1,), (0,)), ((), ())),
        preferred_element_type=jnp.float32,
    )
    grad_weight = unpermute_blocks(partial_value, "ctx", gather_masks)
    grad_residues = jnp.sum(grad_taps[:, None, :] * decay_terms, axis=2)
    grad_decays = -residues * jnp.sum(
        (grad_taps * positions[None, :])[:, None, :] * decay_terms, axis=2
    )
    grad_weight, grad_residues, grad_decays = summed_over_dp(
        grad_weight, grad_residues, grad_decays
    )
    return (grad_queries, grad_keys, grad_values, grad_weight, grad_residues, grad_decays)


def solution(mesh):
    placed = (
        P("dp", "ctx", None),
        P("dp", "ctx", None),
        P("dp", "ctx", None),
        P("dp", "ctx", None),
        P(None, "ctx"),
        P("ctx", None),
        P("ctx", None),
    )
    return jax.shard_map(
        body,
        mesh=mesh,
        in_specs=placed,
        out_specs=(
            P("dp", None, "ctx"),
            P("dp", None, "ctx"),
            P("dp", None, "ctx"),
            P(None, "ctx"),
            P("ctx", None),
            P("ctx", None),
        ),
        check_vma=False,
    )
```

```python
import math

import jax
import jax.numpy as jnp
from jax import lax
from jax.sharding import PartitionSpec as P

FFT_COLS = 128


HIGHEST = lax.Precision.HIGHEST


def fourier_tables(fft_rows, fft_cols):
    total = fft_rows * fft_cols
    row_index = jnp.arange(fft_rows, dtype=jnp.int32)
    col_index = jnp.arange(fft_cols, dtype=jnp.int32)
    first = (row_index[:, None] * row_index[None, :] % fft_rows).astype(jnp.float32) * (
        2.0 * math.pi / fft_rows
    )
    twist = (row_index[:, None] * col_index[None, :] % total).astype(jnp.float32) * (
        2.0 * math.pi / total
    )
    second = (col_index[:, None] * col_index[None, :] % fft_cols).astype(jnp.float32) * (
        2.0 * math.pi / fft_cols
    )
    return (
        (jnp.cos(first), -jnp.sin(first)),
        (jnp.cos(twist), -jnp.sin(twist)),
        (jnp.cos(second), -jnp.sin(second)),
    )


def complex_product(left_re, left_im, right_re, right_im):
    return (left_re * right_re - left_im * right_im, left_re * right_im + left_im * right_re)


def apply_middle(table_re, table_im, data_re):

    def single(table, data):
        return jnp.einsum("kn,cnm->ckm", table, data, precision=HIGHEST)

    return (single(table_re, data_re), single(table_im, data_re))


def apply_last(table_re, table_im, data_re, data_im):

    def single(data, table):
        return jnp.einsum("ckm,mj->ckj", data, table, precision=HIGHEST)

    return (
        single(data_re, table_re) - single(data_im, table_im),
        single(data_im, table_re) + single(data_re, table_im),
    )


def forward_transform(signal, tables):
    (first_re, first_im), (twist_re, twist_im), (second_re, second_im) = tables
    section_re, section_im = apply_middle(first_re, first_im, signal)
    section_re, section_im = complex_product(section_re, section_im, twist_re, twist_im)
    return apply_last(second_re, second_im, section_re, section_im)


def inverse_transform(spec_re, spec_im, tables):
    (first_re, first_im), (twist_re, twist_im), (second_re, second_im) = tables
    section_re, section_im = apply_last(second_re, -second_im, spec_re, spec_im)
    section_re, section_im = complex_product(section_re, section_im, twist_re, -twist_im)
    result = jnp.einsum("kn,cnm->ckm", first_re, section_re, precision=HIGHEST) + jnp.einsum(
        "kn,cnm->ckm", first_im, section_im, precision=HIGHEST
    )
    total = first_re.shape[0] * second_re.shape[0]
    return result / float(total)


def padded_grid(signal, fft_rows, fft_cols):
    channels, seq_len = signal.shape
    padded = jnp.concatenate(
        [signal, jnp.zeros((channels, fft_rows * fft_cols - seq_len), jnp.float32)], axis=1
    )
    return padded.reshape(channels, fft_rows, fft_cols)


def leading_part(grid, seq_len):
    return grid.reshape(grid.shape[0], -1)[:, :seq_len]


def channels_first(block):
    return block[0].astype(jnp.float32).T


def rounded_sum(terms):
    rounded = lax.optimization_barrier(terms.astype(jnp.bfloat16))
    return jnp.sum(rounded.astype(jnp.float32), axis=0)


def columns_by_position(rows, block_width):
    tok_rows = rows.shape[0]
    blocks = rows.shape[1] // block_width
    pieces = jnp.transpose(rows.reshape(tok_rows, blocks, block_width), (1, 0, 2))
    moved = lax.all_to_all(pieces, "ctx", split_axis=0, concat_axis=0, tiled=True)
    return moved.reshape(blocks * tok_rows, block_width)


def shared_weight(out_weight, masks, tie):
    channels, width = out_weight.shape
    half = width // 2
    core = lax.axis_index("dp") % 2
    piece = lax.dynamic_slice_in_dim(out_weight, core * half, half, axis=1)
    piece, tie = lax.optimization_barrier((piece, tie))
    split = channels // 2
    first = doubling_gather(piece[:split], "ctx", masks).reshape(-1, split, half)
    second = doubling_gather(piece[split:], "ctx", other_masks(masks)).reshape(-1, split, half)
    held = jnp.concatenate([first, second], axis=1)
    other = lax.ppermute(held, "dp", axis_pairs(lax.axis_size("dp"), 1))
    full = jnp.concatenate([held, other], axis=2)
    return full[:, :split], full[:, split:], tie


def matching_columns(rows, blocks, masks):
    tok_rows = rows.shape[0]
    half = rows.shape[1] // (2 * blocks)
    me = lax.axis_index("ctx")
    core = lax.axis_index("dp") % 2
    place = jnp.arange(blocks, dtype=jnp.int32)
    source = jnp.zeros_like(place)
    for step, mask in enumerate(masks):
        source = source | jnp.where(((place >> step) & 1) != 0, mask, 0)
    source = me ^ source
    index = (source[:, None] * 2 + (jnp.arange(2, dtype=jnp.int32)[None, :] ^ core)).reshape(-1)
    halves = jnp.take(rows.reshape(tok_rows, 2 * blocks, half), index, axis=1)
    return halves.reshape(tok_rows, blocks, 2 * half)


def axis_pairs(size, mask):
    return [(index, index ^ mask) for index in range(size)]


def ctx_masks(size):
    bits = [1 << b for b in range(size.bit_length() - 1)]
    low = [m for m in bits if m < 4]
    high = [m for m in bits if m >= 4]
    return tuple(reversed(high[1:])) + tuple(reversed(low[1:])) + tuple(high[:1]) + tuple(low[:1])


def other_masks(masks):
    return masks[:-2] + (masks[-1], masks[-2])


def doubling_gather(block, axis, masks):
    size = lax.axis_size(axis)
    held = block
    for mask in masks:
        held = jnp.concatenate([held, lax.ppermute(held, axis, axis_pairs(size, mask))], axis=0)
    return held


def unpermute_blocks(rows, axis, masks):
    size = lax.axis_size(axis)
    me = lax.axis_index(axis)
    wanted = me ^ jnp.arange(size, dtype=jnp.int32)
    place = jnp.zeros_like(wanted)
    for step, mask in enumerate(masks):
        place = place | (((wanted & mask) != 0).astype(jnp.int32) << step)
    blocks = rows.reshape(size, rows.shape[0] // size, rows.shape[1])
    return jnp.take(blocks, place, axis=0).reshape(rows.shape)


def dp_masks(size):
    bits = [1 << b for b in range(size.bit_length() - 1)]
    return tuple(bits[:1]) + tuple(bits[2:]) + tuple(bits[1:2])


def summed_over_dp(grad_weight, grad_residues, grad_decays):
    size = lax.axis_size("dp")
    width = grad_weight.shape[1]
    extra = jnp.stack([grad_residues.reshape(-1), grad_decays.reshape(-1)])
    extra = jnp.pad(extra, ((0, 0), (0, width - extra.shape[1])))
    rows = grad_weight.shape[0] + 2
    padded_rows = -(-rows // size) * size
    held = jnp.concatenate(
        [grad_weight, extra, jnp.zeros((padded_rows - rows, width), jnp.float32)], axis=0
    )
    me = lax.axis_index("dp")
    masks = dp_masks(size)
    for mask in masks:
        half = held.shape[0] // 2
        low, high = held[:half], held[half:]
        upper = (me & mask) != 0
        keep = jnp.where(upper, high, low)
        send = jnp.where(upper, low, high)
        held = keep + lax.ppermute(send, "dp", axis_pairs(size, mask))
    for mask in reversed(masks):
        other = lax.ppermute(held, "dp", axis_pairs(size, mask))
        upper = (me & mask) != 0
        held = jnp.where(upper, jnp.concatenate([other, held]), jnp.concatenate([held, other]))
    count = grad_residues.size
    weight = held[: grad_weight.shape[0]]
    residue_sum = held[grad_weight.shape[0], :count].reshape(grad_residues.shape)
    decay_sum = held[grad_weight.shape[0] + 1, :count].reshape(grad_decays.shape)
    return weight, residue_sum, decay_sum


def body(queries, keys, values, grad_out, out_weight, residues, decays):
    channels = out_weight.shape[0]
    block_width = out_weight.shape[1]
    tok_rows = grad_out.shape[1]
    ctx_size = lax.axis_size("ctx")
    gather_masks = ctx_masks(ctx_size)
    query_ch, key_ch, value_ch = (
        lax.all_to_all(queries, "ctx", split_axis=2, concat_axis=1, tiled=True),
        lax.all_to_all(keys, "ctx", split_axis=2, concat_axis=1, tiled=True),
        lax.all_to_all(values, "ctx", split_axis=2, concat_axis=1, tiled=True),
    )
    weight_first, weight_second, (query_ch, key_ch, value_ch) = shared_weight(
        out_weight, gather_masks, (query_ch, key_ch, value_ch)
    )
    blocks = weight_first.shape[0]
    terms = jnp.concatenate(
        [
            jnp.einsum(
                "tks,kcs->ktc",
                matching_columns(grad_out[0], blocks, order),
                part,
                preferred_element_type=jnp.float32,
            )
            for order, part in ((gather_masks, weight_first), (other_masks(gather_masks), weight_second))
        ],
        axis=2,
    )
    gated_sum = rounded_sum(terms)
    grad_gated = gated_sum.astype(jnp.bfloat16)[None]
    gated_grad_ch = lax.all_to_all(grad_gated, "ctx", split_axis=2, concat_axis=1, tiled=True)
    grad_in, _ = lax.optimization_barrier((grad_out[0], weight_first))
    grad_cols = columns_by_position(grad_in, block_width)
    grad_gated_full = channels_first(gated_grad_ch)
    seq_len = query_ch.shape[1]
    fft_rows = 2 * seq_len // FFT_COLS
    tables = fourier_tables(fft_rows, FFT_COLS)
    query_full = channels_first(query_ch)
    key_full = channels_first(key_ch)
    value_full = channels_first(value_ch)
    positions = jnp.arange(seq_len).astype(jnp.float32)
    decay_terms = jnp.exp(-decays[:, :, None] * positions[None, None, :])
    filter_taps = jnp.sum(residues[:, :, None] * decay_terms, axis=1)
    product = key_full * value_full
    grad_conv = grad_gated_full * query_full
    prod_re, prod_im = forward_transform(padded_grid(product, fft_rows, FFT_COLS), tables)
    taps_re, taps_im = forward_transform(padded_grid(filter_taps, fft_rows, FFT_COLS), tables)
    grad_re, grad_im = forward_transform(padded_grid(grad_conv, fft_rows, FFT_COLS), tables)
    conv_out = leading_part(
        inverse_transform(*complex_product(prod_re, prod_im, taps_re, taps_im), tables), seq_len
    )
    grad_product = leading_part(
        inverse_transform(*complex_product(taps_re, -taps_im, grad_re, grad_im), tables), seq_len
    )
    grad_taps = leading_part(
        inverse_transform(*complex_product(prod_re, -prod_im, grad_re, grad_im), tables), seq_len
    )
    gated_t = (query_full * conv_out).astype(jnp.bfloat16)
    grad_queries = (grad_gated_full * conv_out).T.astype(jnp.bfloat16)[None]
    grad_keys = (grad_product * value_full).T.astype(jnp.bfloat16)[None]
    grad_values = (grad_product * key_full).T.astype(jnp.bfloat16)[None]
    gated_t, grad_cols = lax.optimization_barrier((gated_t, grad_cols))
    split = gated_t.shape[0] // 2
    pieces = []
    for rows, order in ((gated_t[:split], gather_masks), (gated_t[split:], other_masks(gather_masks))):
        partial_value = lax.dot_general(
            doubling_gather(rows, "ctx", order),
            grad_cols,
            (((1,), (0,)), ((), ())),
            preferred_element_type=jnp.float32,
        )
        pieces.append(unpermute_blocks(partial_value, "ctx", order))
    width = grad_cols.shape[1]
    grad_weight = jnp.stack(
        [piece.reshape(ctx_size, split, width) for piece in pieces], axis=1
    ).reshape(-1, width)
    grad_residues = jnp.sum(grad_taps[:, None, :] * decay_terms, axis=2)
    grad_decays = -residues * jnp.sum(
        (grad_taps * positions[None, :])[:, None, :] * decay_terms, axis=2
    )
    grad_weight, grad_residues, grad_decays = summed_over_dp(
        grad_weight, grad_residues, grad_decays
    )
    return (grad_queries, grad_keys, grad_values, grad_weight, grad_residues, grad_decays)


def solution(mesh):
    placed = (
        P("dp", "ctx", None),
        P("dp", "ctx", None),
        P("dp", "ctx", None),
        P("dp", "ctx", None),
        P(None, "ctx"),
        P("ctx", None),
        P("ctx", None),
    )
    return jax.shard_map(
        body,
        mesh=mesh,
        in_specs=placed,
        out_specs=(
            P("dp", None, "ctx"),
            P("dp", None, "ctx"),
            P("dp", None, "ctx"),
            P(None, "ctx"),
            P("ctx", None),
            P("ctx", None),
        ),
        check_vma=False,
    )
```

```python
import math

import jax
import jax.numpy as jnp
from jax import lax
from jax.sharding import PartitionSpec as P

FFT_COLS = 128


HIGHEST = lax.Precision.HIGHEST


def fourier_tables(fft_rows, fft_cols):
    total = fft_rows * fft_cols
    row_index = jnp.arange(fft_rows, dtype=jnp.int32)
    col_index = jnp.arange(fft_cols, dtype=jnp.int32)
    first = (row_index[:, None] * row_index[None, :] % fft_rows).astype(jnp.float32) * (
        2.0 * math.pi / fft_rows
    )
    twist = (row_index[:, None] * col_index[None, :] % total).astype(jnp.float32) * (
        2.0 * math.pi / total
    )
    second = (col_index[:, None] * col_index[None, :] % fft_cols).astype(jnp.float32) * (
        2.0 * math.pi / fft_cols
    )
    return (
        (jnp.cos(first), -jnp.sin(first)),
        (jnp.cos(twist), -jnp.sin(twist)),
        (jnp.cos(second), -jnp.sin(second)),
    )


def complex_product(left_re, left_im, right_re, right_im):
    return (left_re * right_re - left_im * right_im, left_re * right_im + left_im * right_re)


def apply_middle(table_re, table_im, data_re):

    def single(table, data):
        return jnp.einsum("kn,cnm->ckm", table, data, precision=HIGHEST)

    return (single(table_re, data_re), single(table_im, data_re))


def apply_last(table_re, table_im, data_re, data_im):

    def single(data, table):
        return jnp.einsum("ckm,mj->ckj", data, table, precision=HIGHEST)

    return (
        single(data_re, table_re) - single(data_im, table_im),
        single(data_im, table_re) + single(data_re, table_im),
    )


def forward_transform(signal, tables):
    (first_re, first_im), (twist_re, twist_im), (second_re, second_im) = tables
    section_re, section_im = apply_middle(first_re, first_im, signal)
    section_re, section_im = complex_product(section_re, section_im, twist_re, twist_im)
    return apply_last(second_re, second_im, section_re, section_im)


def inverse_transform(spec_re, spec_im, tables):
    (first_re, first_im), (twist_re, twist_im), (second_re, second_im) = tables
    section_re, section_im = apply_last(second_re, -second_im, spec_re, spec_im)
    section_re, section_im = complex_product(section_re, section_im, twist_re, -twist_im)
    result = jnp.einsum("kn,cnm->ckm", first_re, section_re, precision=HIGHEST) + jnp.einsum(
        "kn,cnm->ckm", first_im, section_im, precision=HIGHEST
    )
    total = first_re.shape[0] * second_re.shape[0]
    return result / float(total)


def padded_grid(signal, fft_rows, fft_cols):
    channels, seq_len = signal.shape
    padded = jnp.concatenate(
        [signal, jnp.zeros((channels, fft_rows * fft_cols - seq_len), jnp.float32)], axis=1
    )
    return padded.reshape(channels, fft_rows, fft_cols)


def leading_part(grid, seq_len):
    return grid.reshape(grid.shape[0], -1)[:, :seq_len]


def channels_first(block):
    return block[0].astype(jnp.float32).T


def rounded_sum(terms):
    rounded = lax.optimization_barrier(terms.astype(jnp.bfloat16))
    return jnp.sum(rounded.astype(jnp.float32), axis=0)


def columns_by_position(rows, block_width):
    tok_rows = rows.shape[0]
    blocks = rows.shape[1] // block_width
    pieces = jnp.transpose(rows.reshape(tok_rows, blocks, block_width), (1, 0, 2))
    moved = lax.all_to_all(pieces, "ctx", split_axis=0, concat_axis=0, tiled=True)
    return moved.reshape(blocks * tok_rows, block_width)


def shared_weight(out_weight, masks, tie):
    channels, width = out_weight.shape
    half = width // 2
    core = lax.axis_index("dp") % 2
    piece = lax.dynamic_slice_in_dim(out_weight, core * half, half, axis=1)
    piece, tie = lax.optimization_barrier((piece, tie))
    split = channels // 2
    first = doubling_gather(piece[:split], "ctx", masks).reshape(-1, split, half)
    second = doubling_gather(piece[split:], "ctx", other_masks(masks)).reshape(-1, split, half)
    held = jnp.concatenate([first, second], axis=1)
    other = lax.ppermute(held, "dp", axis_pairs(lax.axis_size("dp"), 1))
    full = jnp.concatenate([held, other], axis=2)
    return full[:, :split], full[:, split:], tie


def matching_columns(rows, blocks, masks):
    tok_rows = rows.shape[0]
    half = rows.shape[1] // (2 * blocks)
    me = lax.axis_index("ctx")
    core = lax.axis_index("dp") % 2
    place = jnp.arange(blocks, dtype=jnp.int32)
    source = jnp.zeros_like(place)
    for step, mask in enumerate(masks):
        source = source | jnp.where(((place >> step) & 1) != 0, mask, 0)
    source = me ^ source
    index = (source[:, None] * 2 + (jnp.arange(2, dtype=jnp.int32)[None, :] ^ core)).reshape(-1)
    halves = jnp.take(rows.reshape(tok_rows, 2 * blocks, half), index, axis=1)
    return halves.reshape(tok_rows, blocks, 2 * half)


def axis_pairs(size, mask):
    return [(index, index ^ mask) for index in range(size)]


def ctx_masks(size):
    bits = [1 << b for b in range(size.bit_length() - 1)]
    low = [m for m in bits if m < 4]
    high = [m for m in bits if m >= 4]
    return tuple(reversed(high[1:])) + tuple(reversed(low[1:])) + tuple(high[:1]) + tuple(low[:1])


def other_masks(masks):
    return masks[:-2] + (masks[-1], masks[-2])


def doubling_gather(block, axis, masks):
    size = lax.axis_size(axis)
    held = block
    for mask in masks:
        held = jnp.concatenate([held, lax.ppermute(held, axis, axis_pairs(size, mask))], axis=0)
    return held


def unpermute_blocks(rows, axis, masks):
    size = lax.axis_size(axis)
    me = lax.axis_index(axis)
    wanted = me ^ jnp.arange(size, dtype=jnp.int32)
    place = jnp.zeros_like(wanted)
    for step, mask in enumerate(masks):
        place = place | (((wanted & mask) != 0).astype(jnp.int32) << step)
    blocks = rows.reshape(size, rows.shape[0] // size, rows.shape[1])
    return jnp.take(blocks, place, axis=0).reshape(rows.shape)


def dp_masks(size):
    bits = [1 << b for b in range(size.bit_length() - 1)]
    return tuple(bits[:1]) + tuple(bits[2:]) + tuple(bits[1:2])


def summed_over_dp(grad_weight, grad_residues, grad_decays):
    size = lax.axis_size("dp")
    width = grad_weight.shape[1]
    extra = jnp.stack([grad_residues.reshape(-1), grad_decays.reshape(-1)])
    extra = jnp.pad(extra, ((0, 0), (0, width - extra.shape[1])))
    rows = grad_weight.shape[0] + 2
    padded_rows = -(-rows // size) * size
    held = jnp.concatenate(
        [grad_weight, extra, jnp.zeros((padded_rows - rows, width), jnp.float32)], axis=0
    )
    me = lax.axis_index("dp")
    masks = dp_masks(size)
    for mask in masks:
        half = held.shape[0] // 2
        low, high = held[:half], held[half:]
        upper = (me & mask) != 0
        keep = jnp.where(upper, high, low)
        send = jnp.where(upper, low, high)
        held = keep + lax.ppermute(send, "dp", axis_pairs(size, mask))
    for mask in reversed(masks):
        other = lax.ppermute(held, "dp", axis_pairs(size, mask))
        upper = (me & mask) != 0
        held = jnp.where(upper, jnp.concatenate([other, held]), jnp.concatenate([held, other]))
    count = grad_residues.size
    weight = held[: grad_weight.shape[0]]
    residue_sum = held[grad_weight.shape[0], :count].reshape(grad_residues.shape)
    decay_sum = held[grad_weight.shape[0] + 1, :count].reshape(grad_decays.shape)
    return weight, residue_sum, decay_sum


def body(queries, keys, values, grad_out, out_weight, residues, decays):
    channels = out_weight.shape[0]
    block_width = out_weight.shape[1]
    tok_rows = grad_out.shape[1]
    ctx_size = lax.axis_size("ctx")
    gather_masks = ctx_masks(ctx_size)
    query_ch, key_ch, value_ch = lax.all_to_all(
        jnp.stack([queries, keys, values]), "ctx", split_axis=3, concat_axis=2, tiled=True
    )
    weight_first, weight_second, (query_ch, key_ch, value_ch) = shared_weight(
        out_weight, gather_masks, (query_ch, key_ch, value_ch)
    )
    blocks = weight_first.shape[0]
    terms = jnp.concatenate(
        [
            jnp.einsum(
                "tks,kcs->ktc",
                matching_columns(grad_out[0], blocks, order),
                part,
                preferred_element_type=jnp.float32,
            )
            for order, part in ((gather_masks, weight_first), (other_masks(gather_masks), weight_second))
        ],
        axis=2,
    )
    gated_sum = rounded_sum(terms)
    grad_gated = gated_sum.astype(jnp.bfloat16)[None]
    gated_grad_ch = lax.all_to_all(grad_gated, "ctx", split_axis=2, concat_axis=1, tiled=True)
    grad_cols = columns_by_position(grad_out[0], block_width)
    grad_gated_full = channels_first(gated_grad_ch)
    seq_len = query_ch.shape[1]
    fft_rows = 2 * seq_len // FFT_COLS
    tables = fourier_tables(fft_rows, FFT_COLS)
    query_full = channels_first(query_ch)
    key_full = channels_first(key_ch)
    value_full = channels_first(value_ch)
    positions = jnp.arange(seq_len).astype(jnp.float32)
    decay_terms = jnp.exp(-decays[:, :, None] * positions[None, None, :])
    filter_taps = jnp.sum(residues[:, :, None] * decay_terms, axis=1)
    product = key_full * value_full
    grad_conv = grad_gated_full * query_full
    prod_re, prod_im = forward_transform(padded_grid(product, fft_rows, FFT_COLS), tables)
    taps_re, taps_im = forward_transform(padded_grid(filter_taps, fft_rows, FFT_COLS), tables)
    grad_re, grad_im = forward_transform(padded_grid(grad_conv, fft_rows, FFT_COLS), tables)
    conv_out = leading_part(
        inverse_transform(*complex_product(prod_re, prod_im, taps_re, taps_im), tables), seq_len
    )
    grad_product = leading_part(
        inverse_transform(*complex_product(taps_re, -taps_im, grad_re, grad_im), tables), seq_len
    )
    grad_taps = leading_part(
        inverse_transform(*complex_product(prod_re, -prod_im, grad_re, grad_im), tables), seq_len
    )
    gated_t = (query_full * conv_out).astype(jnp.bfloat16)
    grad_queries = (grad_gated_full * conv_out).T.astype(jnp.bfloat16)[None]
    grad_keys = (grad_product * value_full).T.astype(jnp.bfloat16)[None]
    grad_values = (grad_product * key_full).T.astype(jnp.bfloat16)[None]
    gated_t, grad_cols = lax.optimization_barrier((gated_t, grad_cols))
    split = gated_t.shape[0] // 2
    pieces = []
    for rows, order in ((gated_t[:split], gather_masks), (gated_t[split:], other_masks(gather_masks))):
        partial_value = lax.dot_general(
            doubling_gather(rows, "ctx", order),
            grad_cols,
            (((1,), (0,)), ((), ())),
            preferred_element_type=jnp.float32,
        )
        pieces.append(unpermute_blocks(partial_value, "ctx", order))
    width = grad_cols.shape[1]
    grad_weight = jnp.stack(
        [piece.reshape(ctx_size, split, width) for piece in pieces], axis=1
    ).reshape(-1, width)
    grad_residues = jnp.sum(grad_taps[:, None, :] * decay_terms, axis=2)
    grad_decays = -residues * jnp.sum(
        (grad_taps * positions[None, :])[:, None, :] * decay_terms, axis=2
    )
    grad_weight, grad_residues, grad_decays = summed_over_dp(
        grad_weight, grad_residues, grad_decays
    )
    return (grad_queries, grad_keys, grad_values, grad_weight, grad_residues, grad_decays)


def solution(mesh):
    placed = (
        P("dp", "ctx", None),
        P("dp", "ctx", None),
        P("dp", "ctx", None),
        P("dp", "ctx", None),
        P(None, "ctx"),
        P("ctx", None),
        P("ctx", None),
    )
    return jax.shard_map(
        body,
        mesh=mesh,
        in_specs=placed,
        out_specs=(
            P("dp", None, "ctx"),
            P("dp", None, "ctx"),
            P("dp", None, "ctx"),
            P(None, "ctx"),
            P("ctx", None),
            P("ctx", None),
        ),
        check_vma=False,
    )
```

```python
import math

import jax
import jax.numpy as jnp
from jax import lax
from jax.sharding import PartitionSpec as P

FFT_COLS = 128


HIGHEST = lax.Precision.HIGHEST


def fourier_tables(fft_rows, fft_cols):
    total = fft_rows * fft_cols
    row_index = jnp.arange(fft_rows, dtype=jnp.int32)
    col_index = jnp.arange(fft_cols, dtype=jnp.int32)
    first = (row_index[:, None] * row_index[None, :] % fft_rows).astype(jnp.float32) * (
        2.0 * math.pi / fft_rows
    )
    twist = (row_index[:, None] * col_index[None, :] % total).astype(jnp.float32) * (
        2.0 * math.pi / total
    )
    second = (col_index[:, None] * col_index[None, :] % fft_cols).astype(jnp.float32) * (
        2.0 * math.pi / fft_cols
    )
    return (
        (jnp.cos(first), -jnp.sin(first)),
        (jnp.cos(twist), -jnp.sin(twist)),
        (jnp.cos(second), -jnp.sin(second)),
    )


def complex_product(left_re, left_im, right_re, right_im):
    return (left_re * right_re - left_im * right_im, left_re * right_im + left_im * right_re)


def apply_middle(table_re, table_im, data_re):

    def single(table, data):
        return jnp.einsum("kn,cnm->ckm", table, data, precision=HIGHEST)

    return (single(table_re, data_re), single(table_im, data_re))


def apply_last(table_re, table_im, data_re, data_im):

    def single(data, table):
        return jnp.einsum("ckm,mj->ckj", data, table, precision=HIGHEST)

    return (
        single(data_re, table_re) - single(data_im, table_im),
        single(data_im, table_re) + single(data_re, table_im),
    )


def forward_transform(signal, tables):
    (first_re, first_im), (twist_re, twist_im), (second_re, second_im) = tables
    section_re, section_im = apply_middle(first_re, first_im, signal)
    section_re, section_im = complex_product(section_re, section_im, twist_re, twist_im)
    return apply_last(second_re, second_im, section_re, section_im)


def inverse_transform(spec_re, spec_im, tables):
    (first_re, first_im), (twist_re, twist_im), (second_re, second_im) = tables
    section_re, section_im = apply_last(second_re, -second_im, spec_re, spec_im)
    section_re, section_im = complex_product(section_re, section_im, twist_re, -twist_im)
    result = jnp.einsum("kn,cnm->ckm", first_re, section_re, precision=HIGHEST) + jnp.einsum(
        "kn,cnm->ckm", first_im, section_im, precision=HIGHEST
    )
    total = first_re.shape[0] * second_re.shape[0]
    return result / float(total)


def padded_grid(signal, fft_rows, fft_cols):
    channels, seq_len = signal.shape
    padded = jnp.concatenate(
        [signal, jnp.zeros((channels, fft_rows * fft_cols - seq_len), jnp.float32)], axis=1
    )
    return padded.reshape(channels, fft_rows, fft_cols)


def leading_part(grid, seq_len):
    return grid.reshape(grid.shape[0], -1)[:, :seq_len]


def channels_first(block):
    return block[0].astype(jnp.float32).T


def rounded_sum(terms):
    rounded = lax.optimization_barrier(terms.astype(jnp.bfloat16))
    return jnp.sum(rounded.astype(jnp.float32), axis=0)


def columns_by_position(rows, block_width):
    tok_rows = rows.shape[0]
    blocks = rows.shape[1] // block_width
    pieces = jnp.transpose(rows.reshape(tok_rows, blocks, block_width), (1, 0, 2))
    moved = lax.all_to_all(pieces, "ctx", split_axis=0, concat_axis=0, tiled=True)
    return moved.reshape(blocks * tok_rows, block_width)


def shared_weight(out_weight, masks, tie):
    channels, width = out_weight.shape
    half = width // 2
    core = lax.axis_index("dp") % 2
    piece = lax.dynamic_slice_in_dim(out_weight, core * half, half, axis=1)
    piece, tie = lax.optimization_barrier((piece, tie))
    split = channels // 2
    first = doubling_gather(piece[:split], "ctx", masks).reshape(-1, split, half)
    second = doubling_gather(piece[split:], "ctx", other_masks(masks)).reshape(-1, split, half)
    held = jnp.concatenate([first, second], axis=1)
    other = lax.ppermute(held, "dp", axis_pairs(lax.axis_size("dp"), 1))
    full = jnp.concatenate([held, other], axis=2)
    return full[:, :split], full[:, split:], tie


def matching_columns(rows, blocks, masks):
    tok_rows = rows.shape[0]
    half = rows.shape[1] // (2 * blocks)
    me = lax.axis_index("ctx")
    core = lax.axis_index("dp") % 2
    place = jnp.arange(blocks, dtype=jnp.int32)
    source = jnp.zeros_like(place)
    for step, mask in enumerate(masks):
        source = source | jnp.where(((place >> step) & 1) != 0, mask, 0)
    source = me ^ source
    index = (source[:, None] * 2 + (jnp.arange(2, dtype=jnp.int32)[None, :] ^ core)).reshape(-1)
    halves = jnp.take(rows.reshape(tok_rows, 2 * blocks, half), index, axis=1)
    return halves.reshape(tok_rows, blocks, 2 * half)


def axis_pairs(size, mask):
    return [(index, index ^ mask) for index in range(size)]


def ctx_masks(size):
    bits = [1 << b for b in range(size.bit_length() - 1)]
    low = [m for m in bits if m < 4]
    high = [m for m in bits if m >= 4]
    return tuple(reversed(high[1:])) + tuple(reversed(low[1:])) + tuple(high[:1]) + tuple(low[:1])


def other_masks(masks):
    return masks[:-2] + (masks[-1], masks[-2])


def doubling_gather(block, axis, masks):
    size = lax.axis_size(axis)
    held = block
    for mask in masks:
        held = jnp.concatenate([held, lax.ppermute(held, axis, axis_pairs(size, mask))], axis=0)
    return held


def unpermute_blocks(rows, axis, masks):
    size = lax.axis_size(axis)
    me = lax.axis_index(axis)
    wanted = me ^ jnp.arange(size, dtype=jnp.int32)
    place = jnp.zeros_like(wanted)
    for step, mask in enumerate(masks):
        place = place | (((wanted & mask) != 0).astype(jnp.int32) << step)
    blocks = rows.reshape(size, rows.shape[0] // size, rows.shape[1])
    return jnp.take(blocks, place, axis=0).reshape(rows.shape)


def dp_groups(size):
    bits = [1 << b for b in range(size.bit_length() - 1)]
    return ((bits[2], bits[3]), (bits[0], bits[1]))


def group_partner(pair, offset):
    return (pair[0] if offset & 1 else 0) | (pair[1] if offset & 2 else 0)


def summed_over_dp(grad_weight, grad_residues, grad_decays):
    size = lax.axis_size("dp")
    width = grad_weight.shape[1]
    extra = jnp.stack([grad_residues.reshape(-1), grad_decays.reshape(-1)])
    extra = jnp.pad(extra, ((0, 0), (0, width - extra.shape[1])))
    rows = grad_weight.shape[0] + 2
    padded_rows = -(-rows // size) * size
    held = jnp.concatenate(
        [grad_weight, extra, jnp.zeros((padded_rows - rows, width), jnp.float32)], axis=0
    )
    me = lax.axis_index("dp")
    groups = dp_groups(size)
    for pair in groups:
        mine = ((me & pair[0]) != 0).astype(jnp.int32) + 2 * ((me & pair[1]) != 0).astype(jnp.int32)
        quarters = held.reshape(4, held.shape[0] // 4, width)
        total = jnp.take(quarters, mine, axis=0)
        for offset in (1, 2, 3):
            send = jnp.take(quarters, mine ^ offset, axis=0)
            total = total + lax.ppermute(send, "dp", axis_pairs(size, group_partner(pair, offset)))
        held = total
    for pair in reversed(groups):
        mine = ((me & pair[0]) != 0).astype(jnp.int32) + 2 * ((me & pair[1]) != 0).astype(jnp.int32)
        arrived = [held] + [
            lax.ppermute(held, "dp", axis_pairs(size, group_partner(pair, offset)))
            for offset in (1, 2, 3)
        ]
        held = jnp.take(jnp.stack(arrived), jnp.arange(4, dtype=jnp.int32) ^ mine, axis=0)
        held = held.reshape(-1, width)
    count = grad_residues.size
    weight = held[: grad_weight.shape[0]]
    residue_sum = held[grad_weight.shape[0], :count].reshape(grad_residues.shape)
    decay_sum = held[grad_weight.shape[0] + 1, :count].reshape(grad_decays.shape)
    return weight, residue_sum, decay_sum


def body(queries, keys, values, grad_out, out_weight, residues, decays):
    channels = out_weight.shape[0]
    block_width = out_weight.shape[1]
    tok_rows = grad_out.shape[1]
    ctx_size = lax.axis_size("ctx")
    gather_masks = ctx_masks(ctx_size)
    query_ch, key_ch, value_ch = lax.all_to_all(
        jnp.stack([queries, keys, values]), "ctx", split_axis=3, concat_axis=2, tiled=True
    )
    weight_first, weight_second, (query_ch, key_ch, value_ch) = shared_weight(
        out_weight, gather_masks, (query_ch, key_ch, value_ch)
    )
    blocks = weight_first.shape[0]
    terms = jnp.concatenate(
        [
            jnp.einsum(
                "tks,kcs->ktc",
                matching_columns(grad_out[0], blocks, order),
                part,
                preferred_element_type=jnp.float32,
            )
            for order, part in ((gather_masks, weight_first), (other_masks(gather_masks), weight_second))
        ],
        axis=2,
    )
    gated_sum = rounded_sum(terms)
    grad_gated = gated_sum.astype(jnp.bfloat16)[None]
    gated_grad_ch = lax.all_to_all(grad_gated, "ctx", split_axis=2, concat_axis=1, tiled=True)
    grad_cols = columns_by_position(grad_out[0], block_width)
    grad_gated_full = channels_first(gated_grad_ch)
    seq_len = query_ch.shape[1]
    fft_rows = 2 * seq_len // FFT_COLS
    tables = fourier_tables(fft_rows, FFT_COLS)
    query_full = channels_first(query_ch)
    key_full = channels_first(key_ch)
    value_full = channels_first(value_ch)
    positions = jnp.arange(seq_len).astype(jnp.float32)
    decay_terms = jnp.exp(-decays[:, :, None] * positions[None, None, :])
    filter_taps = jnp.sum(residues[:, :, None] * decay_terms, axis=1)
    product = key_full * value_full
    grad_conv = grad_gated_full * query_full
    prod_re, prod_im = forward_transform(padded_grid(product, fft_rows, FFT_COLS), tables)
    taps_re, taps_im = forward_transform(padded_grid(filter_taps, fft_rows, FFT_COLS), tables)
    grad_re, grad_im = forward_transform(padded_grid(grad_conv, fft_rows, FFT_COLS), tables)
    conv_out = leading_part(
        inverse_transform(*complex_product(prod_re, prod_im, taps_re, taps_im), tables), seq_len
    )
    grad_product = leading_part(
        inverse_transform(*complex_product(taps_re, -taps_im, grad_re, grad_im), tables), seq_len
    )
    grad_taps = leading_part(
        inverse_transform(*complex_product(prod_re, -prod_im, grad_re, grad_im), tables), seq_len
    )
    gated_t = (query_full * conv_out).astype(jnp.bfloat16)
    grad_queries = (grad_gated_full * conv_out).T.astype(jnp.bfloat16)[None]
    grad_keys = (grad_product * value_full).T.astype(jnp.bfloat16)[None]
    grad_values = (grad_product * key_full).T.astype(jnp.bfloat16)[None]
    gated_t, grad_cols = lax.optimization_barrier((gated_t, grad_cols))
    split = gated_t.shape[0] // 2
    pieces = []
    for rows, order in ((gated_t[:split], gather_masks), (gated_t[split:], other_masks(gather_masks))):
        partial_value = lax.dot_general(
            doubling_gather(rows, "ctx", order),
            grad_cols,
            (((1,), (0,)), ((), ())),
            preferred_element_type=jnp.float32,
        )
        pieces.append(unpermute_blocks(partial_value, "ctx", order))
    width = grad_cols.shape[1]
    grad_weight = jnp.stack(
        [piece.reshape(ctx_size, split, width) for piece in pieces], axis=1
    ).reshape(-1, width)
    grad_residues = jnp.sum(grad_taps[:, None, :] * decay_terms, axis=2)
    grad_decays = -residues * jnp.sum(
        (grad_taps * positions[None, :])[:, None, :] * decay_terms, axis=2
    )
    grad_weight, grad_residues, grad_decays = summed_over_dp(
        grad_weight, grad_residues, grad_decays
    )
    return (grad_queries, grad_keys, grad_values, grad_weight, grad_residues, grad_decays)


def solution(mesh):
    placed = (
        P("dp", "ctx", None),
        P("dp", "ctx", None),
        P("dp", "ctx", None),
        P("dp", "ctx", None),
        P(None, "ctx"),
        P("ctx", None),
        P("ctx", None),
    )
    return jax.shard_map(
        body,
        mesh=mesh,
        in_specs=placed,
        out_specs=(
            P("dp", None, "ctx"),
            P("dp", None, "ctx"),
            P("dp", None, "ctx"),
            P(None, "ctx"),
            P("ctx", None),
            P("ctx", None),
        ),
        check_vma=False,
    )
```

```python
import math

import jax
import jax.numpy as jnp
from jax import lax
from jax.sharding import PartitionSpec as P

FFT_COLS = 128


HIGHEST = lax.Precision.HIGHEST


def fourier_tables(fft_rows, fft_cols):
    total = fft_rows * fft_cols
    row_index = jnp.arange(fft_rows, dtype=jnp.int32)
    col_index = jnp.arange(fft_cols, dtype=jnp.int32)
    first = (row_index[:, None] * row_index[None, :] % fft_rows).astype(jnp.float32) * (
        2.0 * math.pi / fft_rows
    )
    twist = (row_index[:, None] * col_index[None, :] % total).astype(jnp.float32) * (
        2.0 * math.pi / total
    )
    second = (col_index[:, None] * col_index[None, :] % fft_cols).astype(jnp.float32) * (
        2.0 * math.pi / fft_cols
    )
    return (
        (jnp.cos(first), -jnp.sin(first)),
        (jnp.cos(twist), -jnp.sin(twist)),
        (jnp.cos(second), -jnp.sin(second)),
    )


def complex_product(left_re, left_im, right_re, right_im):
    return (left_re * right_re - left_im * right_im, left_re * right_im + left_im * right_re)


def apply_middle(table_re, table_im, data_re):

    def single(table, data):
        return jnp.einsum("kn,cnm->ckm", table, data, precision=HIGHEST)

    return (single(table_re, data_re), single(table_im, data_re))


def apply_last(table_re, table_im, data_re, data_im):

    def single(data, table):
        return jnp.einsum("ckm,mj->ckj", data, table, precision=HIGHEST)

    return (
        single(data_re, table_re) - single(data_im, table_im),
        single(data_im, table_re) + single(data_re, table_im),
    )


def forward_transform(signal, tables):
    (first_re, first_im), (twist_re, twist_im), (second_re, second_im) = tables
    section_re, section_im = apply_middle(first_re, first_im, signal)
    section_re, section_im = complex_product(section_re, section_im, twist_re, twist_im)
    return apply_last(second_re, second_im, section_re, section_im)


def inverse_transform(spec_re, spec_im, tables):
    (first_re, first_im), (twist_re, twist_im), (second_re, second_im) = tables
    section_re, section_im = apply_last(second_re, -second_im, spec_re, spec_im)
    section_re, section_im = complex_product(section_re, section_im, twist_re, -twist_im)
    result = jnp.einsum("kn,cnm->ckm", first_re, section_re, precision=HIGHEST) + jnp.einsum(
        "kn,cnm->ckm", first_im, section_im, precision=HIGHEST
    )
    total = first_re.shape[0] * second_re.shape[0]
    return result / float(total)


def padded_grid(signal, fft_rows, fft_cols):
    channels, seq_len = signal.shape
    padded = jnp.concatenate(
        [signal, jnp.zeros((channels, fft_rows * fft_cols - seq_len), jnp.float32)], axis=1
    )
    return padded.reshape(channels, fft_rows, fft_cols)


def leading_part(grid, seq_len):
    return grid.reshape(grid.shape[0], -1)[:, :seq_len]


def channels_first(block):
    return block[0].astype(jnp.float32).T


def rounded_sum(terms):
    rounded = lax.optimization_barrier(terms.astype(jnp.bfloat16))
    return jnp.sum(rounded.astype(jnp.float32), axis=0)


def columns_by_position(rows, block_width):
    tok_rows = rows.shape[0]
    blocks = rows.shape[1] // block_width
    pieces = jnp.transpose(rows.reshape(tok_rows, blocks, block_width), (1, 0, 2))
    moved = lax.all_to_all(pieces, "ctx", split_axis=0, concat_axis=0, tiled=True)
    return moved.reshape(blocks * tok_rows, block_width)


def shared_weight(out_weight, masks, tie):
    channels, width = out_weight.shape
    half = width // 2
    core = lax.axis_index("dp") % 2
    piece = lax.dynamic_slice_in_dim(out_weight, core * half, half, axis=1)
    piece, tie = lax.optimization_barrier((piece, tie))
    split = channels // 2
    first, second = paired_gather(piece, "ctx", masks)
    first = first.reshape(-1, split, half)
    second = second.reshape(-1, split, half)
    held = jnp.concatenate([first, second], axis=1)
    other = lax.ppermute(held, "dp", axis_pairs(lax.axis_size("dp"), 1))
    full = jnp.concatenate([held, other], axis=2)
    return full[:, :split], full[:, split:], tie


def matching_columns(rows, blocks, masks):
    tok_rows = rows.shape[0]
    half = rows.shape[1] // (2 * blocks)
    me = lax.axis_index("ctx")
    core = lax.axis_index("dp") % 2
    place = jnp.arange(blocks, dtype=jnp.int32)
    source = jnp.zeros_like(place)
    for step, mask in enumerate(masks):
        source = source | jnp.where(((place >> step) & 1) != 0, mask, 0)
    source = me ^ source
    index = (source[:, None] * 2 + (jnp.arange(2, dtype=jnp.int32)[None, :] ^ core)).reshape(-1)
    halves = jnp.take(rows.reshape(tok_rows, 2 * blocks, half), index, axis=1)
    return halves.reshape(tok_rows, blocks, 2 * half)


def axis_pairs(size, mask):
    return [(index, index ^ mask) for index in range(size)]


def ctx_masks(size):
    bits = [1 << b for b in range(size.bit_length() - 1)]
    low = [m for m in bits if m < 4]
    high = [m for m in bits if m >= 4]
    return tuple(reversed(high[1:])) + tuple(reversed(low[1:])) + tuple(high[:1]) + tuple(low[:1])


def other_masks(masks):
    return masks[:-2] + (masks[-1], masks[-2])


def paired_gather(block, axis, masks):
    size = lax.axis_size(axis)
    rows = block.shape[0]
    held = block
    for mask in masks[:-2]:
        held = jnp.concatenate([held, lax.ppermute(held, axis, axis_pairs(size, mask))], axis=0)
    held = held.reshape(-1, 2, rows // 2, *block.shape[1:])
    first = held[:, 0].reshape(-1, *block.shape[1:])
    second = held[:, 1].reshape(-1, *block.shape[1:])
    for mask, other in zip(masks[-2:], other_masks(masks)[-2:]):
        first = jnp.concatenate([first, lax.ppermute(first, axis, axis_pairs(size, mask))], axis=0)
        second = jnp.concatenate([second, lax.ppermute(second, axis, axis_pairs(size, other))], axis=0)
    return first, second


def doubling_gather(block, axis, masks):
    size = lax.axis_size(axis)
    held = block
    for mask in masks:
        held = jnp.concatenate([held, lax.ppermute(held, axis, axis_pairs(size, mask))], axis=0)
    return held


def unpermute_blocks(rows, axis, masks):
    size = lax.axis_size(axis)
    me = lax.axis_index(axis)
    wanted = me ^ jnp.arange(size, dtype=jnp.int32)
    place = jnp.zeros_like(wanted)
    for step, mask in enumerate(masks):
        place = place | (((wanted & mask) != 0).astype(jnp.int32) << step)
    blocks = rows.reshape(size, rows.shape[0] // size, rows.shape[1])
    return jnp.take(blocks, place, axis=0).reshape(rows.shape)


def dp_masks(size):
    bits = [1 << b for b in range(size.bit_length() - 1)]
    return tuple(bits[:1]) + tuple(bits[2:]) + tuple(bits[1:2])


def summed_over_dp(grad_weight, grad_residues, grad_decays):
    size = lax.axis_size("dp")
    width = grad_weight.shape[1]
    extra = jnp.stack([grad_residues.reshape(-1), grad_decays.reshape(-1)])
    extra = jnp.pad(extra, ((0, 0), (0, width - extra.shape[1])))
    rows = grad_weight.shape[0] + 2
    padded_rows = -(-rows // size) * size
    held = jnp.concatenate(
        [grad_weight, extra, jnp.zeros((padded_rows - rows, width), jnp.float32)], axis=0
    )
    me = lax.axis_index("dp")
    masks = dp_masks(size)
    for mask in masks:
        half = held.shape[0] // 2
        low, high = held[:half], held[half:]
        upper = (me & mask) != 0
        keep = jnp.where(upper, high, low)
        send = jnp.where(upper, low, high)
        held = keep + lax.ppermute(send, "dp", axis_pairs(size, mask))
    for mask in reversed(masks):
        other = lax.ppermute(held, "dp", axis_pairs(size, mask))
        upper = (me & mask) != 0
        held = jnp.where(upper, jnp.concatenate([other, held]), jnp.concatenate([held, other]))
    count = grad_residues.size
    weight = held[: grad_weight.shape[0]]
    residue_sum = held[grad_weight.shape[0], :count].reshape(grad_residues.shape)
    decay_sum = held[grad_weight.shape[0] + 1, :count].reshape(grad_decays.shape)
    return weight, residue_sum, decay_sum


def body(queries, keys, values, grad_out, out_weight, residues, decays):
    channels = out_weight.shape[0]
    block_width = out_weight.shape[1]
    tok_rows = grad_out.shape[1]
    ctx_size = lax.axis_size("ctx")
    gather_masks = ctx_masks(ctx_size)
    query_ch, key_ch, value_ch = lax.all_to_all(
        jnp.stack([queries, keys, values]), "ctx", split_axis=3, concat_axis=2, tiled=True
    )
    weight_first, weight_second, (query_ch, key_ch, value_ch) = shared_weight(
        out_weight, gather_masks, (query_ch, key_ch, value_ch)
    )
    blocks = weight_first.shape[0]
    terms = jnp.concatenate(
        [
            jnp.einsum(
                "tks,kcs->ktc",
                matching_columns(grad_out[0], blocks, order),
                part,
                preferred_element_type=jnp.float32,
            )
            for order, part in ((gather_masks, weight_first), (other_masks(gather_masks), weight_second))
        ],
        axis=2,
    )
    gated_sum = rounded_sum(terms)
    grad_gated = gated_sum.astype(jnp.bfloat16)[None]
    gated_grad_ch = lax.all_to_all(grad_gated, "ctx", split_axis=2, concat_axis=1, tiled=True)
    grad_cols = columns_by_position(grad_out[0], block_width)
    grad_gated_full = channels_first(gated_grad_ch)
    seq_len = query_ch.shape[1]
    fft_rows = 2 * seq_len // FFT_COLS
    tables = fourier_tables(fft_rows, FFT_COLS)
    query_full = channels_first(query_ch)
    key_full = channels_first(key_ch)
    value_full = channels_first(value_ch)
    positions = jnp.arange(seq_len).astype(jnp.float32)
    decay_terms = jnp.exp(-decays[:, :, None] * positions[None, None, :])
    filter_taps = jnp.sum(residues[:, :, None] * decay_terms, axis=1)
    product = key_full * value_full
    grad_conv = grad_gated_full * query_full
    prod_re, prod_im = forward_transform(padded_grid(product, fft_rows, FFT_COLS), tables)
    taps_re, taps_im = forward_transform(padded_grid(filter_taps, fft_rows, FFT_COLS), tables)
    grad_re, grad_im = forward_transform(padded_grid(grad_conv, fft_rows, FFT_COLS), tables)
    conv_out = leading_part(
        inverse_transform(*complex_product(prod_re, prod_im, taps_re, taps_im), tables), seq_len
    )
    grad_product = leading_part(
        inverse_transform(*complex_product(taps_re, -taps_im, grad_re, grad_im), tables), seq_len
    )
    grad_taps = leading_part(
        inverse_transform(*complex_product(prod_re, -prod_im, grad_re, grad_im), tables), seq_len
    )
    gated_t = (query_full * conv_out).astype(jnp.bfloat16)
    grad_queries = (grad_gated_full * conv_out).T.astype(jnp.bfloat16)[None]
    grad_keys = (grad_product * value_full).T.astype(jnp.bfloat16)[None]
    grad_values = (grad_product * key_full).T.astype(jnp.bfloat16)[None]
    gated_t, grad_cols = lax.optimization_barrier((gated_t, grad_cols))
    split = gated_t.shape[0] // 2
    pieces = []
    halves = paired_gather(gated_t, "ctx", gather_masks)
    for rows, order in zip(halves, (gather_masks, other_masks(gather_masks))):
        partial_value = lax.dot_general(
            rows,
            grad_cols,
            (((1,), (0,)), ((), ())),
            preferred_element_type=jnp.float32,
        )
        pieces.append(unpermute_blocks(partial_value, "ctx", order))
    width = grad_cols.shape[1]
    grad_weight = jnp.stack(
        [piece.reshape(ctx_size, split, width) for piece in pieces], axis=1
    ).reshape(-1, width)
    grad_residues = jnp.sum(grad_taps[:, None, :] * decay_terms, axis=2)
    grad_decays = -residues * jnp.sum(
        (grad_taps * positions[None, :])[:, None, :] * decay_terms, axis=2
    )
    grad_weight, grad_residues, grad_decays = summed_over_dp(
        grad_weight, grad_residues, grad_decays
    )
    return (grad_queries, grad_keys, grad_values, grad_weight, grad_residues, grad_decays)


def solution(mesh):
    placed = (
        P("dp", "ctx", None),
        P("dp", "ctx", None),
        P("dp", "ctx", None),
        P("dp", "ctx", None),
        P(None, "ctx"),
        P("ctx", None),
        P("ctx", None),
    )
    return jax.shard_map(
        body,
        mesh=mesh,
        in_specs=placed,
        out_specs=(
            P("dp", None, "ctx"),
            P("dp", None, "ctx"),
            P("dp", None, "ctx"),
            P(None, "ctx"),
            P("ctx", None),
            P("ctx", None),
        ),
        check_vma=False,
    )
```

```python
import math

import jax
import jax.numpy as jnp
from jax import lax
from jax.sharding import PartitionSpec as P

FFT_COLS = 128


HIGHEST = lax.Precision.HIGHEST


def fourier_tables(fft_rows, fft_cols):
    total = fft_rows * fft_cols
    row_index = jnp.arange(fft_rows, dtype=jnp.int32)
    col_index = jnp.arange(fft_cols, dtype=jnp.int32)
    first = (row_index[:, None] * row_index[None, :] % fft_rows).astype(jnp.float32) * (
        2.0 * math.pi / fft_rows
    )
    twist = (row_index[:, None] * col_index[None, :] % total).astype(jnp.float32) * (
        2.0 * math.pi / total
    )
    second = (col_index[:, None] * col_index[None, :] % fft_cols).astype(jnp.float32) * (
        2.0 * math.pi / fft_cols
    )
    return (
        (jnp.cos(first), -jnp.sin(first)),
        (jnp.cos(twist), -jnp.sin(twist)),
        (jnp.cos(second), -jnp.sin(second)),
    )


def complex_product(left_re, left_im, right_re, right_im):
    return (left_re * right_re - left_im * right_im, left_re * right_im + left_im * right_re)


def apply_middle(table_re, table_im, data_re):

    def single(table, data):
        return jnp.einsum("kn,cnm->ckm", table, data, precision=HIGHEST)

    return (single(table_re, data_re), single(table_im, data_re))


def apply_last(table_re, table_im, data_re, data_im):

    def single(data, table):
        return jnp.einsum("ckm,mj->ckj", data, table, precision=HIGHEST)

    return (
        single(data_re, table_re) - single(data_im, table_im),
        single(data_im, table_re) + single(data_re, table_im),
    )


def forward_transform(signal, tables):
    (first_re, first_im), (twist_re, twist_im), (second_re, second_im) = tables
    section_re, section_im = apply_middle(first_re, first_im, signal)
    section_re, section_im = complex_product(section_re, section_im, twist_re, twist_im)
    return apply_last(second_re, second_im, section_re, section_im)


def inverse_transform(spec_re, spec_im, tables):
    (first_re, first_im), (twist_re, twist_im), (second_re, second_im) = tables
    section_re, section_im = apply_last(second_re, -second_im, spec_re, spec_im)
    section_re, section_im = complex_product(section_re, section_im, twist_re, -twist_im)
    result = jnp.einsum("kn,cnm->ckm", first_re, section_re, precision=HIGHEST) + jnp.einsum(
        "kn,cnm->ckm", first_im, section_im, precision=HIGHEST
    )
    total = first_re.shape[0] * second_re.shape[0]
    return result / float(total)


def padded_grid(signal, fft_rows, fft_cols):
    channels, seq_len = signal.shape
    padded = jnp.concatenate(
        [signal, jnp.zeros((channels, fft_rows * fft_cols - seq_len), jnp.float32)], axis=1
    )
    return padded.reshape(channels, fft_rows, fft_cols)


def leading_part(grid, seq_len):
    return grid.reshape(grid.shape[0], -1)[:, :seq_len]


def channels_first(block):
    return block[0].astype(jnp.float32).T


def rounded_sum(terms):
    rounded = lax.optimization_barrier(terms.astype(jnp.bfloat16))
    return jnp.sum(rounded.astype(jnp.float32), axis=0)


def columns_by_position(rows, block_width):
    tok_rows = rows.shape[0]
    blocks = rows.shape[1] // block_width
    pieces = jnp.transpose(rows.reshape(tok_rows, blocks, block_width), (1, 0, 2))
    moved = lax.all_to_all(pieces, "ctx", split_axis=0, concat_axis=0, tiled=True)
    return moved.reshape(blocks * tok_rows, block_width)


def shared_weight(out_weight, masks, tie):
    channels, width = out_weight.shape
    half = width // 2
    core = lax.axis_index("dp") % 2
    piece = lax.dynamic_slice_in_dim(out_weight, core * half, half, axis=1)
    piece, tie = lax.optimization_barrier((piece, tie))
    split = channels // 2
    first = doubling_gather(piece[:split], "ctx", masks).reshape(-1, split, half)
    second = doubling_gather(piece[split:], "ctx", other_masks(masks)).reshape(-1, split, half)
    held = jnp.concatenate([first, second], axis=1)
    other = lax.ppermute(held, "dp", axis_pairs(lax.axis_size("dp"), 1))
    full = jnp.concatenate([held, other], axis=2)
    return full[:, :split], full[:, split:], tie


def matching_columns(rows, blocks, masks):
    tok_rows = rows.shape[0]
    half = rows.shape[1] // (2 * blocks)
    me = lax.axis_index("ctx")
    core = lax.axis_index("dp") % 2
    place = jnp.arange(blocks, dtype=jnp.int32)
    source = jnp.zeros_like(place)
    for step, mask in enumerate(masks):
        source = source | jnp.where(((place >> step) & 1) != 0, mask, 0)
    source = me ^ source
    index = (source[:, None] * 2 + (jnp.arange(2, dtype=jnp.int32)[None, :] ^ core)).reshape(-1)
    halves = jnp.take(rows.reshape(tok_rows, 2 * blocks, half), index, axis=1)
    return halves.reshape(tok_rows, blocks, 2 * half)


def axis_pairs(size, mask):
    return [(index, index ^ mask) for index in range(size)]


def ctx_masks(size):
    bits = [1 << b for b in range(size.bit_length() - 1)]
    low = [m for m in bits if m < 4]
    high = [m for m in bits if m >= 4]
    return tuple(reversed(high[1:])) + tuple(reversed(low[1:])) + tuple(high[:1]) + tuple(low[:1])


def other_masks(masks):
    return masks[:-2] + (masks[-1], masks[-2])


def paired_gather(block, axis, masks):
    size = lax.axis_size(axis)
    rows = block.shape[0]
    held = block
    for mask in masks[:-2]:
        held = jnp.concatenate([held, lax.ppermute(held, axis, axis_pairs(size, mask))], axis=0)
    held = held.reshape(-1, 2, rows // 2, *block.shape[1:])
    first = held[:, 0].reshape(-1, *block.shape[1:])
    second = held[:, 1].reshape(-1, *block.shape[1:])
    for mask, other in zip(masks[-2:], other_masks(masks)[-2:]):
        first = jnp.concatenate([first, lax.ppermute(first, axis, axis_pairs(size, mask))], axis=0)
        second = jnp.concatenate([second, lax.ppermute(second, axis, axis_pairs(size, other))], axis=0)
    return first, second


def doubling_gather(block, axis, masks):
    size = lax.axis_size(axis)
    held = block
    for mask in masks:
        held = jnp.concatenate([held, lax.ppermute(held, axis, axis_pairs(size, mask))], axis=0)
    return held


def unpermute_blocks(rows, axis, masks):
    size = lax.axis_size(axis)
    me = lax.axis_index(axis)
    wanted = me ^ jnp.arange(size, dtype=jnp.int32)
    place = jnp.zeros_like(wanted)
    for step, mask in enumerate(masks):
        place = place | (((wanted & mask) != 0).astype(jnp.int32) << step)
    blocks = rows.reshape(size, rows.shape[0] // size, rows.shape[1])
    return jnp.take(blocks, place, axis=0).reshape(rows.shape)


def dp_masks(size):
    bits = [1 << b for b in range(size.bit_length() - 1)]
    return tuple(bits[:1]) + tuple(bits[2:]) + tuple(bits[1:2])


def summed_over_dp(grad_weight, grad_residues, grad_decays):
    size = lax.axis_size("dp")
    width = grad_weight.shape[1]
    extra = jnp.stack([grad_residues.reshape(-1), grad_decays.reshape(-1)])
    extra = jnp.pad(extra, ((0, 0), (0, width - extra.shape[1])))
    rows = grad_weight.shape[0] + 2
    padded_rows = -(-rows // size) * size
    held = jnp.concatenate(
        [grad_weight, extra, jnp.zeros((padded_rows - rows, width), jnp.float32)], axis=0
    )
    me = lax.axis_index("dp")
    masks = dp_masks(size)
    for mask in masks:
        half = held.shape[0] // 2
        low, high = held[:half], held[half:]
        upper = (me & mask) != 0
        keep = jnp.where(upper, high, low)
        send = jnp.where(upper, low, high)
        held = keep + lax.ppermute(send, "dp", axis_pairs(size, mask))
    for mask in reversed(masks):
        other = lax.ppermute(held, "dp", axis_pairs(size, mask))
        upper = (me & mask) != 0
        held = jnp.where(upper, jnp.concatenate([other, held]), jnp.concatenate([held, other]))
    count = grad_residues.size
    weight = held[: grad_weight.shape[0]]
    residue_sum = held[grad_weight.shape[0], :count].reshape(grad_residues.shape)
    decay_sum = held[grad_weight.shape[0] + 1, :count].reshape(grad_decays.shape)
    return weight, residue_sum, decay_sum


def body(queries, keys, values, grad_out, out_weight, residues, decays):
    channels = out_weight.shape[0]
    block_width = out_weight.shape[1]
    tok_rows = grad_out.shape[1]
    ctx_size = lax.axis_size("ctx")
    gather_masks = ctx_masks(ctx_size)
    query_ch, key_ch, value_ch = lax.all_to_all(
        jnp.stack([queries, keys, values]), "ctx", split_axis=3, concat_axis=2, tiled=True
    )
    weight_first, weight_second, (query_ch, key_ch, value_ch) = shared_weight(
        out_weight, gather_masks, (query_ch, key_ch, value_ch)
    )
    blocks = weight_first.shape[0]
    terms = jnp.concatenate(
        [
            jnp.einsum(
                "tks,kcs->ktc",
                matching_columns(grad_out[0], blocks, order),
                part,
                preferred_element_type=jnp.float32,
            )
            for order, part in ((gather_masks, weight_first), (other_masks(gather_masks), weight_second))
        ],
        axis=2,
    )
    gated_sum = rounded_sum(terms)
    grad_gated = gated_sum.astype(jnp.bfloat16)[None]
    gated_grad_ch = lax.all_to_all(grad_gated, "ctx", split_axis=2, concat_axis=1, tiled=True)
    grad_cols = columns_by_position(grad_out[0], block_width)
    grad_gated_full = channels_first(gated_grad_ch)
    seq_len = query_ch.shape[1]
    fft_rows = 2 * seq_len // FFT_COLS
    tables = fourier_tables(fft_rows, FFT_COLS)
    query_full = channels_first(query_ch)
    key_full = channels_first(key_ch)
    value_full = channels_first(value_ch)
    positions = jnp.arange(seq_len).astype(jnp.float32)
    decay_terms = jnp.exp(-decays[:, :, None] * positions[None, None, :])
    filter_taps = jnp.sum(residues[:, :, None] * decay_terms, axis=1)
    product = key_full * value_full
    grad_conv = grad_gated_full * query_full
    prod_re, prod_im = forward_transform(padded_grid(product, fft_rows, FFT_COLS), tables)
    taps_re, taps_im = forward_transform(padded_grid(filter_taps, fft_rows, FFT_COLS), tables)
    grad_re, grad_im = forward_transform(padded_grid(grad_conv, fft_rows, FFT_COLS), tables)
    conv_out = leading_part(
        inverse_transform(*complex_product(prod_re, prod_im, taps_re, taps_im), tables), seq_len
    )
    grad_product = leading_part(
        inverse_transform(*complex_product(taps_re, -taps_im, grad_re, grad_im), tables), seq_len
    )
    grad_taps = leading_part(
        inverse_transform(*complex_product(prod_re, -prod_im, grad_re, grad_im), tables), seq_len
    )
    gated_t = (query_full * conv_out).astype(jnp.bfloat16)
    grad_queries = (grad_gated_full * conv_out).T.astype(jnp.bfloat16)[None]
    grad_keys = (grad_product * value_full).T.astype(jnp.bfloat16)[None]
    grad_values = (grad_product * key_full).T.astype(jnp.bfloat16)[None]
    gated_t, grad_cols = lax.optimization_barrier((gated_t, grad_cols))
    split = gated_t.shape[0] // 2
    pieces = []
    halves = paired_gather(gated_t, "ctx", gather_masks)
    for rows, order in zip(halves, (gather_masks, other_masks(gather_masks))):
        partial_value = lax.dot_general(
            rows,
            grad_cols,
            (((1,), (0,)), ((), ())),
            preferred_element_type=jnp.float32,
        )
        pieces.append(unpermute_blocks(partial_value, "ctx", order))
    width = grad_cols.shape[1]
    grad_weight = jnp.stack(
        [piece.reshape(ctx_size, split, width) for piece in pieces], axis=1
    ).reshape(-1, width)
    grad_residues = jnp.sum(grad_taps[:, None, :] * decay_terms, axis=2)
    grad_decays = -residues * jnp.sum(
        (grad_taps * positions[None, :])[:, None, :] * decay_terms, axis=2
    )
    grad_weight, grad_residues, grad_decays = summed_over_dp(
        grad_weight, grad_residues, grad_decays
    )
    return (grad_queries, grad_keys, grad_values, grad_weight, grad_residues, grad_decays)


def solution(mesh):
    placed = (
        P("dp", "ctx", None),
        P("dp", "ctx", None),
        P("dp", "ctx", None),
        P("dp", "ctx", None),
        P(None, "ctx"),
        P("ctx", None),
        P("ctx", None),
    )
    return jax.shard_map(
        body,
        mesh=mesh,
        in_specs=placed,
        out_specs=(
            P("dp", None, "ctx"),
            P("dp", None, "ctx"),
            P("dp", None, "ctx"),
            P(None, "ctx"),
            P("ctx", None),
            P("ctx", None),
        ),
        check_vma=False,
    )
```

```python
import math

import jax
import jax.numpy as jnp
from jax import lax
from jax.sharding import PartitionSpec as P

FFT_COLS = 128


HIGHEST = lax.Precision.HIGHEST


def fourier_tables(fft_rows, fft_cols):
    total = fft_rows * fft_cols
    row_index = jnp.arange(fft_rows, dtype=jnp.int32)
    col_index = jnp.arange(fft_cols, dtype=jnp.int32)
    first = (row_index[:, None] * row_index[None, :] % fft_rows).astype(jnp.float32) * (
        2.0 * math.pi / fft_rows
    )
    twist = (row_index[:, None] * col_index[None, :] % total).astype(jnp.float32) * (
        2.0 * math.pi / total
    )
    second = (col_index[:, None] * col_index[None, :] % fft_cols).astype(jnp.float32) * (
        2.0 * math.pi / fft_cols
    )
    return (
        (jnp.cos(first), -jnp.sin(first)),
        (jnp.cos(twist), -jnp.sin(twist)),
        (jnp.cos(second), -jnp.sin(second)),
    )


def complex_product(left_re, left_im, right_re, right_im):
    return (left_re * right_re - left_im * right_im, left_re * right_im + left_im * right_re)


def apply_middle(table_re, table_im, data_re):

    def single(table, data):
        return jnp.einsum("kn,cnm->ckm", table, data, precision=HIGHEST)

    return (single(table_re, data_re), single(table_im, data_re))


def apply_last(table_re, table_im, data_re, data_im):

    def single(data, table):
        return jnp.einsum("ckm,mj->ckj", data, table, precision=HIGHEST)

    return (
        single(data_re, table_re) - single(data_im, table_im),
        single(data_im, table_re) + single(data_re, table_im),
    )


def forward_transform(signal, tables):
    (first_re, first_im), (twist_re, twist_im), (second_re, second_im) = tables
    section_re, section_im = apply_middle(first_re, first_im, signal)
    section_re, section_im = complex_product(section_re, section_im, twist_re, twist_im)
    return apply_last(second_re, second_im, section_re, section_im)


def inverse_transform(spec_re, spec_im, tables):
    (first_re, first_im), (twist_re, twist_im), (second_re, second_im) = tables
    section_re, section_im = apply_last(second_re, -second_im, spec_re, spec_im)
    section_re, section_im = complex_product(section_re, section_im, twist_re, -twist_im)
    result = jnp.einsum("kn,cnm->ckm", first_re, section_re, precision=HIGHEST) + jnp.einsum(
        "kn,cnm->ckm", first_im, section_im, precision=HIGHEST
    )
    total = first_re.shape[0] * second_re.shape[0]
    return result / float(total)


def padded_grid(signal, fft_rows, fft_cols):
    channels, seq_len = signal.shape
    padded = jnp.concatenate(
        [signal, jnp.zeros((channels, fft_rows * fft_cols - seq_len), jnp.float32)], axis=1
    )
    return padded.reshape(channels, fft_rows, fft_cols)


def leading_part(grid, seq_len):
    return grid.reshape(grid.shape[0], -1)[:, :seq_len]


def channels_first(block):
    return block[0].astype(jnp.float32).T


def rounded_sum(terms):
    rounded = lax.optimization_barrier(terms.astype(jnp.bfloat16))
    return jnp.sum(rounded.astype(jnp.float32), axis=0)


def columns_by_position(rows, block_width):
    tok_rows = rows.shape[0]
    blocks = rows.shape[1] // block_width
    pieces = jnp.transpose(rows.reshape(tok_rows, blocks, block_width), (1, 0, 2))
    moved = lax.all_to_all(pieces, "ctx", split_axis=0, concat_axis=0, tiled=True)
    return moved.reshape(blocks * tok_rows, block_width)


def shared_weight(out_weight, masks, tie):
    channels, width = out_weight.shape
    half = width // 2
    core = lax.axis_index("dp") % 2
    piece = lax.dynamic_slice_in_dim(out_weight, core * half, half, axis=1)
    piece, tie = lax.optimization_barrier((piece, tie))
    split = channels // 2
    first = doubling_gather(piece[:split], "ctx", masks).reshape(-1, split, half)
    second = doubling_gather(piece[split:], "ctx", other_masks(masks)).reshape(-1, split, half)
    held = jnp.concatenate([first, second], axis=1)
    other = lax.ppermute(held, "dp", axis_pairs(lax.axis_size("dp"), 1))
    full = jnp.concatenate([held, other], axis=2)
    return full[:, :split], full[:, split:], tie


def matching_columns(rows, blocks, masks):
    tok_rows = rows.shape[0]
    half = rows.shape[1] // (2 * blocks)
    me = lax.axis_index("ctx")
    core = lax.axis_index("dp") % 2
    place = jnp.arange(blocks, dtype=jnp.int32)
    source = jnp.zeros_like(place)
    for step, mask in enumerate(masks):
        source = source | jnp.where(((place >> step) & 1) != 0, mask, 0)
    source = me ^ source
    index = (source[:, None] * 2 + (jnp.arange(2, dtype=jnp.int32)[None, :] ^ core)).reshape(-1)
    halves = jnp.take(rows.reshape(tok_rows, 2 * blocks, half), index, axis=1)
    return halves.reshape(tok_rows, blocks, 2 * half)


def axis_pairs(size, mask):
    return [(index, index ^ mask) for index in range(size)]


def ctx_masks(size):
    bits = [1 << b for b in range(size.bit_length() - 1)]
    low = [m for m in bits if m < 4]
    high = [m for m in bits if m >= 4]
    return tuple(reversed(high[1:])) + tuple(reversed(low[1:])) + tuple(high[:1]) + tuple(low[:1])


def other_masks(masks):
    return masks[:-2] + (masks[-1], masks[-2])


def paired_gather(block, axis, masks):
    size = lax.axis_size(axis)
    rows = block.shape[0]
    held = block
    for mask in masks[:-2]:
        held = jnp.concatenate([held, lax.ppermute(held, axis, axis_pairs(size, mask))], axis=0)
    held = held.reshape(-1, 2, rows // 2, *block.shape[1:])
    first = held[:, 0].reshape(-1, *block.shape[1:])
    second = held[:, 1].reshape(-1, *block.shape[1:])
    for mask, other in zip(masks[-2:], other_masks(masks)[-2:]):
        first = jnp.concatenate([first, lax.ppermute(first, axis, axis_pairs(size, mask))], axis=0)
        second = jnp.concatenate([second, lax.ppermute(second, axis, axis_pairs(size, other))], axis=0)
    return first, second


def doubling_gather(block, axis, masks):
    size = lax.axis_size(axis)
    held = block
    for mask in masks:
        held = jnp.concatenate([held, lax.ppermute(held, axis, axis_pairs(size, mask))], axis=0)
    return held


def unpermute_blocks(rows, axis, masks):
    size = lax.axis_size(axis)
    me = lax.axis_index(axis)
    wanted = me ^ jnp.arange(size, dtype=jnp.int32)
    place = jnp.zeros_like(wanted)
    for step, mask in enumerate(masks):
        place = place | (((wanted & mask) != 0).astype(jnp.int32) << step)
    blocks = rows.reshape(size, rows.shape[0] // size, rows.shape[1])
    return jnp.take(blocks, place, axis=0).reshape(rows.shape)


def dp_masks(size):
    bits = [1 << b for b in range(size.bit_length() - 1)]
    return tuple(bits[:1]) + tuple(bits[2:]) + tuple(bits[1:2])


def summed_over_dp(grad_weight, grad_residues, grad_decays):
    size = lax.axis_size("dp")
    width = grad_weight.shape[1]
    extra = jnp.stack([grad_residues.reshape(-1), grad_decays.reshape(-1)])
    extra = jnp.pad(extra, ((0, 0), (0, width - extra.shape[1])))
    rows = grad_weight.shape[0] + 2
    padded_rows = -(-rows // size) * size
    held = jnp.concatenate(
        [grad_weight, extra, jnp.zeros((padded_rows - rows, width), jnp.float32)], axis=0
    )
    me = lax.axis_index("dp")
    masks = dp_masks(size)
    for mask in masks:
        half = held.shape[0] // 2
        low, high = held[:half], held[half:]
        upper = (me & mask) != 0
        keep = jnp.where(upper, high, low)
        send = jnp.where(upper, low, high)
        held = keep + lax.ppermute(send, "dp", axis_pairs(size, mask))
    for mask in reversed(masks):
        other = lax.ppermute(held, "dp", axis_pairs(size, mask))
        upper = (me & mask) != 0
        held = jnp.where(upper, jnp.concatenate([other, held]), jnp.concatenate([held, other]))
    count = grad_residues.size
    weight = held[: grad_weight.shape[0]]
    residue_sum = held[grad_weight.shape[0], :count].reshape(grad_residues.shape)
    decay_sum = held[grad_weight.shape[0] + 1, :count].reshape(grad_decays.shape)
    return weight, residue_sum, decay_sum


def body(queries, keys, values, grad_out, out_weight, residues, decays):
    channels = out_weight.shape[0]
    block_width = out_weight.shape[1]
    tok_rows = grad_out.shape[1]
    ctx_size = lax.axis_size("ctx")
    gather_masks = ctx_masks(ctx_size)
    query_ch, key_ch, value_ch = lax.all_to_all(
        jnp.stack([queries, keys, values]), "ctx", split_axis=3, concat_axis=2, tiled=True
    )
    weight_first, weight_second, (query_ch, key_ch, value_ch) = shared_weight(
        out_weight, gather_masks, (query_ch, key_ch, value_ch)
    )
    blocks = weight_first.shape[0]
    terms = jnp.concatenate(
        [
            jnp.einsum(
                "tks,kcs->ktc",
                matching_columns(grad_out[0], blocks, order),
                part,
                preferred_element_type=jnp.float32,
            )
            for order, part in ((gather_masks, weight_first), (other_masks(gather_masks), weight_second))
        ],
        axis=2,
    )
    gated_sum = rounded_sum(terms)
    grad_gated = gated_sum.astype(jnp.bfloat16)[None]
    gated_grad_ch = lax.all_to_all(grad_gated, "ctx", split_axis=2, concat_axis=1, tiled=True)
    grad_cols = columns_by_position(grad_out[0], block_width)
    grad_gated_full = channels_first(gated_grad_ch)
    seq_len = query_ch.shape[1]
    fft_rows = 2 * seq_len // FFT_COLS
    tables = fourier_tables(fft_rows, FFT_COLS)
    query_full = channels_first(query_ch)
    key_full = channels_first(key_ch)
    value_full = channels_first(value_ch)
    positions = jnp.arange(seq_len).astype(jnp.float32)
    decay_terms = jnp.exp(-decays[:, :, None] * positions[None, None, :])
    filter_taps = jnp.sum(residues[:, :, None] * decay_terms, axis=1)
    product = key_full * value_full
    grad_conv = grad_gated_full * query_full
    prod_re, prod_im = forward_transform(padded_grid(product, fft_rows, FFT_COLS), tables)
    taps_re, taps_im = forward_transform(padded_grid(filter_taps, fft_rows, FFT_COLS), tables)
    grad_re, grad_im = forward_transform(padded_grid(grad_conv, fft_rows, FFT_COLS), tables)
    conv_out = leading_part(
        inverse_transform(*complex_product(prod_re, prod_im, taps_re, taps_im), tables), seq_len
    )
    product_re, product_im = complex_product(taps_re, -taps_im, grad_re, grad_im)
    lag_re, lag_im = complex_product(prod_re, -prod_im, grad_re, grad_im)
    both = leading_part(
        inverse_transform(
            jnp.concatenate([product_re, lag_re]), jnp.concatenate([product_im, lag_im]), tables
        ),
        seq_len,
    )
    grad_product, grad_taps = both[: product_re.shape[0]], both[product_re.shape[0] :]
    gated_t = (query_full * conv_out).astype(jnp.bfloat16)
    grad_queries = (grad_gated_full * conv_out).T.astype(jnp.bfloat16)[None]
    grad_keys = (grad_product * value_full).T.astype(jnp.bfloat16)[None]
    grad_values = (grad_product * key_full).T.astype(jnp.bfloat16)[None]
    gated_t, grad_cols = lax.optimization_barrier((gated_t, grad_cols))
    split = gated_t.shape[0] // 2
    pieces = []
    halves = paired_gather(gated_t, "ctx", gather_masks)
    for rows, order in zip(halves, (gather_masks, other_masks(gather_masks))):
        partial_value = lax.dot_general(
            rows,
            grad_cols,
            (((1,), (0,)), ((), ())),
            preferred_element_type=jnp.float32,
        )
        pieces.append(unpermute_blocks(partial_value, "ctx", order))
    width = grad_cols.shape[1]
    grad_weight = jnp.stack(
        [piece.reshape(ctx_size, split, width) for piece in pieces], axis=1
    ).reshape(-1, width)
    grad_residues = jnp.sum(grad_taps[:, None, :] * decay_terms, axis=2)
    grad_decays = -residues * jnp.sum(
        (grad_taps * positions[None, :])[:, None, :] * decay_terms, axis=2
    )
    grad_weight, grad_residues, grad_decays = summed_over_dp(
        grad_weight, grad_residues, grad_decays
    )
    return (grad_queries, grad_keys, grad_values, grad_weight, grad_residues, grad_decays)


def solution(mesh):
    placed = (
        P("dp", "ctx", None),
        P("dp", "ctx", None),
        P("dp", "ctx", None),
        P("dp", "ctx", None),
        P(None, "ctx"),
        P("ctx", None),
        P("ctx", None),
    )
    return jax.shard_map(
        body,
        mesh=mesh,
        in_specs=placed,
        out_specs=(
            P("dp", None, "ctx"),
            P("dp", None, "ctx"),
            P("dp", None, "ctx"),
            P(None, "ctx"),
            P("ctx", None),
            P("ctx", None),
        ),
        check_vma=False,
    )
```
